32 devices in a mesh: grp: 2 (over x), seq: 16 (over z, y, core).
Axes of the slice: x: 2, y: 2, z: 4, core: 2. Of those that a mesh axis runs over, the one named last changes fastest.
Arguments:
- queries: bfloat16 [4096, 4096], P(('grp', 'seq')), parts along dimension 0, may hold values from -5.2 to 5.2
- key_rows: bfloat16 [4096, 4096], P(('grp', 'seq')), parts along dimension 0, may hold values from -5.2 to 5.2
- values: bfloat16 [4096, 4096], P(('grp', 'seq')), parts along dimension 0, may hold values from -6 to 6
- random_ids: int32 [32, 3], P('grp'), parts along dimension 0, may hold values from 0 to 15
- global_ids: int32 [4], P('grp'), parts along dimension 0, may hold values from 0 to 15
Outputs:
- attended: bfloat16 [4096, 4096], P(('grp', 'seq')), parts along dimension 0
The draws below stay inside these ranges and needn't reach their ends.
There are 2 independent parts, one for each index of `grp`. The reference program is written for one: setup_inputs(seed, part) draws one part's arguments, and reference() takes and returns one part's arrays. A program takes and returns all parts, laid end to end along the dimension named above; each array names one. Nothing has to cross between parts.
All inputs are finite; a program needn't handle non-finite values.
Results may differ from the reference program's by a relative error of at most 0.0047.
Values may be sent and summed in bfloat16 or wider, within the bound.
No kernel may reach another device: no remote copies, remote signals or barrier semaphores. Data moves between devices by JAX's collectives and lax.ppermute only.
A program may use at most 128 MiB of HBM per device.

```python
import math
import jax
import jax.numpy as jnp
import numpy as np
from jax import lax

HEADS = 32
HEAD_DIM = 128
BLK = 128
RAND = 3
GLOBAL = 2
NB = 16
TOKENS = 2048


def paired_draw(key):
    feat_width = HEADS * HEAD_DIM
    full_shape = (TOKENS, feat_width)
    query_key = jax.random.fold_in(key, 101)
    row_key = jax.random.fold_in(key, 102)
    queries_out = jnp.clip(jax.random.normal(query_key, full_shape, jnp.float32), -4.0, 4.0)
    rows_out = jnp.clip(jax.random.normal(row_key, full_shape, jnp.float32), -4.0, 4.0)
    return (queries_out, rows_out)


def draw_queries(key, part):
    return paired_draw(key)[0].astype(jnp.bfloat16)


def draw_key_rows(key, part):
    return paired_draw(key)[1].astype(jnp.bfloat16)


def with_ends(values, key, smallest, largest):
    extent = values.shape
    index_at = [jax.random.randint(jax.random.fold_in(key, axis), (), 0, extent[axis]) for axis in range(len(extent))]
    values = values.at[tuple(index_at)].set(smallest)
    longest = extent.index(max(extent))
    index_at[longest] = (index_at[longest] + 1) % extent[longest]
    return values.at[tuple(index_at)].set(largest)


def block_scale(rng, shape, pieces, least, high):
    factor_of = 1.0
    for dim, shards_of in pieces:
        steps = jax.random.uniform(jax.random.fold_in(jax.random.fold_in(rng, 6), dim), (shards_of,), jnp.float32, least / len(pieces), high / len(pieces))
        factor_of = factor_of * jnp.repeat(jnp.exp(steps), shape[dim] // shards_of).reshape((-1,) + (1,) * (len(shape) - 1 - dim))
    return factor_of


def cumulative_ranks(number_of, skew):
    weights = [(1 << 20) // math.isqrt(rank ** skew) + 1 for rank in range(1, number_of + 1)]
    deviation = 1 + sum(weights) // (1 << 30)
    return np.cumsum(np.array([max(1, weight // deviation) for weight in weights]))


def skewed_ids(key, extent, amount, lean):
    table = cumulative_ranks(amount, lean)
    lot = jax.random.randint(jax.random.fold_in(key, 1), extent, 0, int(table[amount - 1]))
    grade = jnp.searchsorted(jnp.asarray(table, jnp.int32), lot, side="right")
    return jax.random.permutation(jax.random.fold_in(key, 2), amount)[grade].astype(jnp.int32)


def bell_draw(stream_key, dims, deviation, reach, split=(), kind=jnp.bfloat16):
    gain = block_scale(stream_key, dims, split, -0.22, 0.18) if split else 1.0
    values = jax.random.normal(stream_key, dims, jnp.float32) * deviation * gain
    return jnp.minimum(jnp.maximum(values, -reach), reach).astype(kind)


def setup_inputs(seed: int = 0, part: int = 0) -> dict:
    seeds = jax.random.split(jax.random.key(seed), 6)
    own_keys = jax.random.split(jax.random.fold_in(seeds[5], part), 6)
    return {
        "queries": draw_queries(jax.random.fold_in(jax.random.fold_in(seeds[5], part), 71), part),
        "key_rows": draw_key_rows(jax.random.fold_in(jax.random.fold_in(seeds[5], part), 71), part),
        "values": bell_draw(own_keys[2], (TOKENS, HEADS * HEAD_DIM), 1.0, 6.0, ((0, 16),)),
        "random_ids": with_ends(skewed_ids(own_keys[3], (NB, RAND), NB, 2), jax.random.fold_in(own_keys[3], 3), 0, NB - 1).astype(jnp.int32),
        "global_ids": jax.random.randint(own_keys[4], (GLOBAL,), 0, NB).astype(jnp.int32),
    }


neg_big = -1e+30

def reference(queries, key_rows, values, random_ids, global_ids):
    query_blocks = queries.reshape(NB, BLK, HEADS, HEAD_DIM)
    key_blocks = key_rows.reshape(NB, BLK, HEADS, HEAD_DIM)
    value_blocks = values.reshape(NB, BLK, HEADS, HEAD_DIM)
    factor = 1.0 / math.sqrt(HEAD_DIM)

    def attend_one(block_index):
        window_ids = block_index + jnp.arange(-1, 2, dtype=jnp.int32)
        block_ids = jnp.concatenate((window_ids, global_ids.astype(jnp.int32), random_ids[block_index].astype(jnp.int32)))
        usable = (block_ids >= 0) & (block_ids < NB)
        clipped = jnp.clip(block_ids, 0, NB - 1)
        picked_keys = key_blocks[clipped].reshape(-1, HEADS, HEAD_DIM)
        picked_values = value_blocks[clipped].reshape(-1, HEADS, HEAD_DIM)
        usable_keys = jnp.repeat(usable, BLK)
        scores = jnp.einsum('qhd,khd->hqk', query_blocks[block_index].astype(jnp.float32), picked_keys.astype(jnp.float32)) * factor
        scores = jnp.where(usable_keys[None, None, :], scores, neg_big)
        highest = lax.optimization_barrier(jnp.max(scores, axis=-1, keepdims=True))
        weights = jnp.exp(scores - highest)
        denominator = lax.optimization_barrier(jnp.sum(weights, axis=-1))
        rounded = lax.optimization_barrier(weights.astype(jnp.bfloat16)).astype(jnp.float32)
        mixed = jnp.einsum('hqk,khd->qhd', rounded, picked_values.astype(jnp.float32))
        return (mixed / jnp.transpose(denominator)[:, :, None]).astype(jnp.bfloat16)
    result = lax.map(attend_one, jnp.arange(NB, dtype=jnp.int32))
    return result.reshape(TOKENS, HEADS * HEAD_DIM)
```

```python
import functools
import math

import jax
import jax.numpy as jnp
from jax import lax
from jax.experimental import pallas as pl
from jax.experimental.pallas import tpu as pltpu
from jax.sharding import PartitionSpec as P

HEADS = 32
HEAD_DIM = 128
BLK = 128
RAND = 3
GLOBAL = 2
GROUP = 4

neg_big = -1e30


def shifted(block, axis, step):
    count = lax.axis_size(axis)
    if step > 0:
        pairs = [(i, i + 1) for i in range(count - 1)]
    else:
        pairs = [(i + 1, i) for i in range(count - 1)]
    return lax.ppermute(block, axis, pairs)


def attend_kernel(flags_ref, q_ref, own_ref, left_ref, right_ref, far_ref, o_ref, *, factor):
    left_ok = flags_ref[0] > 0
    right_ok = flags_ref[1] > 0
    rows = q_ref.shape[0]
    far_rows = far_ref.shape[1]
    keys = 3 * BLK + far_rows
    col = lax.broadcasted_iota(jnp.int32, (rows, keys), 1)
    bad = ((col < BLK) & jnp.logical_not(left_ok)) | (
        (col >= 2 * BLK) & (col < 3 * BLK) & jnp.logical_not(right_ok)
    )
    for g in range(q_ref.shape[1] // HEAD_DIM):
        sl = pl.ds(g * HEAD_DIM, HEAD_DIM)
        qh = q_ref[:, sl]
        k_all = jnp.concatenate(
            (left_ref[0, :, sl], own_ref[0, :, sl], right_ref[0, :, sl], far_ref[0, :, sl]), axis=0
        )
        scores = (
            lax.dot_general(
                qh, k_all, (((1,), (1,)), ((), ())), preferred_element_type=jnp.float32
            )
            * factor
        )
        scores = jnp.where(bad, neg_big, scores)
        highest = jnp.max(scores, axis=-1, keepdims=True)
        weights = jnp.exp(scores - highest)
        denominator = jnp.sum(weights, axis=-1, keepdims=True)
        v_all = jnp.concatenate(
            (left_ref[1, :, sl], own_ref[1, :, sl], right_ref[1, :, sl], far_ref[1, :, sl]), axis=0
        )
        mixed = jnp.dot(weights.astype(jnp.bfloat16), v_all, preferred_element_type=jnp.float32)
        o_ref[:, sl] = (mixed / denominator).astype(o_ref.dtype)


def attend(flags, queries, own, left, right, far):
    rows, width = queries.shape
    gw = GROUP * HEAD_DIM
    steps = width // gw
    far_rows = far.shape[1]
    kernel = functools.partial(attend_kernel, factor=1.0 / math.sqrt(HEAD_DIM))
    kv_spec = pl.BlockSpec((2, rows, gw), lambda h, f: (0, 0, h))
    return pl.pallas_call(
        kernel,
        out_shape=jax.ShapeDtypeStruct((rows, width), queries.dtype),
        grid_spec=pltpu.PrefetchScalarGridSpec(
            num_scalar_prefetch=1,
            grid=(steps,),
            in_specs=[
                pl.BlockSpec((rows, gw), lambda h, f: (0, h)),
                kv_spec,
                kv_spec,
                kv_spec,
                pl.BlockSpec((2, far_rows, gw), lambda h, f: (0, 0, h)),
            ],
            out_specs=pl.BlockSpec((rows, gw), lambda h, f: (0, h)),
        ),
    )(flags, queries, own, left, right, far)


def per_device(queries, key_rows, values, random_ids, global_ids):
    tok_rows, feat_width = queries.shape
    peers = lax.axis_size("seq")
    my_rank = lax.axis_index("seq")
    local_blocks = tok_rows // BLK
    assert local_blocks == 1
    all_blocks = local_blocks * peers
    keyvals = jnp.stack((key_rows, values))
    spread = lax.all_to_all(keyvals, "seq", split_axis=2, concat_axis=1, tiled=True)
    spread_blocks = spread.reshape(2, all_blocks, BLK, feat_width // peers)
    pick_ids = jnp.concatenate(
        (jnp.broadcast_to(global_ids[None, :], (all_blocks, GLOBAL)), random_ids), axis=1
    )
    picks = GLOBAL + RAND
    outgoing = jnp.take(spread_blocks, pick_ids.reshape(-1), axis=1)
    fetched = lax.all_to_all(outgoing, "seq", split_axis=1, concat_axis=3, tiled=True)
    far = fetched.reshape(2, picks * BLK, feat_width)
    left = shifted(keyvals, "seq", 1)
    right = shifted(keyvals, "seq", -1)
    flags = jnp.stack((my_rank > 0, my_rank < peers - 1)).astype(jnp.int32)
    return attend(flags, queries, keyvals, left, right, far)


def solution(mesh):
    return jax.shard_map(
        per_device,
        mesh=mesh,
        in_specs=(
            P(("grp", "seq"), None),
            P(("grp", "seq"), None),
            P(("grp", "seq"), None),
            P("grp", None),
            P("grp"),
        ),
        out_specs=P(("grp", "seq"), None),
        check_vma=False,
    )
```

```python
import functools
import math

import jax
import jax.numpy as jnp
from jax import lax
from jax.experimental import pallas as pl
from jax.experimental.pallas import tpu as pltpu
from jax.sharding import PartitionSpec as P

HEADS = 32
HEAD_DIM = 128
BLK = 128
RAND = 3
GLOBAL = 2
GROUP = 4

neg_big = -1e30


def shifted(block, axis, step):
    count = lax.axis_size(axis)
    if step > 0:
        pairs = [(i, i + 1) for i in range(count - 1)]
    else:
        pairs = [(i + 1, i) for i in range(count - 1)]
    return lax.ppermute(block, axis, pairs)


def attend_kernel(
    flags_ref, q_ref, own_ref, left_ref, right_ref, glob_ref, rand_ref, o_ref, *, factor
):
    left_ok = flags_ref[0] > 0
    right_ok = flags_ref[1] > 0
    rows = q_ref.shape[0]
    far_count = glob_ref.shape[1] + rand_ref.shape[1]
    keys = (3 + far_count) * BLK
    col = lax.broadcasted_iota(jnp.int32, (rows, keys), 1)
    bad = ((col < BLK) & jnp.logical_not(left_ok)) | (
        (col >= 2 * BLK) & (col < 3 * BLK) & jnp.logical_not(right_ok)
    )
    for g in range(q_ref.shape[1] // HEAD_DIM):
        sl = pl.ds(g * HEAD_DIM, HEAD_DIM)
        qh = q_ref[:, sl]
        k_all = jnp.concatenate(
            (
                left_ref[0, :, sl],
                own_ref[0, :, sl],
                right_ref[0, :, sl],
                *[glob_ref[0, j, 0, :, sl] for j in range(glob_ref.shape[1])],
                *[rand_ref[0, j, 0, :, sl] for j in range(rand_ref.shape[1])],
            ),
            axis=0,
        )
        scores = (
            lax.dot_general(
                qh, k_all, (((1,), (1,)), ((), ())), preferred_element_type=jnp.float32
            )
            * factor
        )
        scores = jnp.where(bad, neg_big, scores)
        highest = jnp.max(scores, axis=-1, keepdims=True)
        weights = jnp.exp(scores - highest)
        denominator = jnp.sum(weights, axis=-1, keepdims=True)
        v_all = jnp.concatenate(
            (
                left_ref[1, :, sl],
                own_ref[1, :, sl],
                right_ref[1, :, sl],
                *[glob_ref[0, j, 1, :, sl] for j in range(glob_ref.shape[1])],
                *[rand_ref[0, j, 1, :, sl] for j in range(rand_ref.shape[1])],
            ),
            axis=0,
        )
        mixed = jnp.dot(weights.astype(jnp.bfloat16), v_all, preferred_element_type=jnp.float32)
        o_ref[:, sl] = (mixed / denominator).astype(o_ref.dtype)


def far_spec(far, gw):
    per = far.shape[4] // gw
    return pl.BlockSpec(
        (1, far.shape[1], 2, BLK, gw), lambda h, f: (h // per, 0, 0, 0, h % per)
    )


def attend(flags, queries, own, left, right, glob, rand, gw):
    rows, width = queries.shape
    steps = width // gw
    kernel = functools.partial(attend_kernel, factor=1.0 / math.sqrt(HEAD_DIM))
    kv_spec = pl.BlockSpec((2, rows, gw), lambda h, f: (0, 0, h))
    return pl.pallas_call(
        kernel,
        out_shape=jax.ShapeDtypeStruct((rows, width), queries.dtype),
        grid_spec=pltpu.PrefetchScalarGridSpec(
            num_scalar_prefetch=1,
            grid=(steps,),
            in_specs=[
                pl.BlockSpec((rows, gw), lambda h, f: (0, h)),
                kv_spec,
                kv_spec,
                kv_spec,
                far_spec(glob, gw),
                far_spec(rand, gw),
            ],
            out_specs=pl.BlockSpec((rows, gw), lambda h, f: (0, h)),
        ),
    )(flags, queries, own, left, right, glob, rand)


def feature_major(far):
    peers, count, two, rows, piece = far.shape
    return far.transpose(1, 2, 3, 0, 4).reshape(1, count, two, rows, peers * piece)


def per_device(queries, key_rows, values, random_ids, global_ids):
    tok_rows, feat_width = queries.shape
    peers = lax.axis_size("seq")
    my_rank = lax.axis_index("seq")
    local_blocks = tok_rows // BLK
    assert local_blocks == 1
    all_blocks = local_blocks * peers
    piece = feat_width // peers
    keyvals = jnp.stack((key_rows, values))
    pieces = keyvals.reshape(2, BLK, peers, piece).transpose(2, 0, 1, 3)
    spread = lax.all_to_all(pieces, "seq", split_axis=0, concat_axis=0, tiled=True)
    glob_piece = jnp.take(spread, global_ids, axis=0, mode="clip")
    glob = lax.all_gather(glob_piece[None], "seq", axis=0, tiled=True)
    outgoing = jnp.take(spread, random_ids.reshape(-1), axis=0, mode="clip")
    outgoing = outgoing.reshape(all_blocks, RAND, 2, BLK, piece)
    rand = lax.all_to_all(outgoing, "seq", split_axis=0, concat_axis=0, tiled=True)
    left = shifted(keyvals, "seq", 1)
    right = shifted(keyvals, "seq", -1)
    flags = jnp.stack((my_rank > 0, my_rank < peers - 1)).astype(jnp.int32)
    if piece % HEAD_DIM == 0:
        gw = piece
    else:
        glob = feature_major(glob)
        rand = feature_major(rand)
        gw = GROUP * HEAD_DIM
    return attend(flags, queries, keyvals, left, right, glob, rand, gw)


def solution(mesh):
    return jax.shard_map(
        per_device,
        mesh=mesh,
        in_specs=(
            P(("grp", "seq"), None),
            P(("grp", "seq"), None),
            P(("grp", "seq"), None),
            P("grp", None),
            P("grp"),
        ),
        out_specs=P(("grp", "seq"), None),
        check_vma=False,
    )
```

```python
import functools
import math

import jax
import jax.numpy as jnp
from jax import lax
from jax.experimental import pallas as pl
from jax.experimental.pallas import tpu as pltpu
from jax.sharding import Mesh, PartitionSpec as P

HEADS = 32
HEAD_DIM = 128
BLK = 128
RAND = 3
GLOBAL = 2
GROUP = 4

neg_big = -1e30


def shifted(block, axis, step, count):
    if step > 0:
        pairs = [(i, i + 1) for i in range(count - 1)]
    else:
        pairs = [(i + 1, i) for i in range(count - 1)]
    return lax.ppermute(block, axis, pairs)


def attend_kernel(
    flags_ref, q_ref, own_ref, left_ref, right_ref, glob_ref, rand_ref, o_ref, *, factor
):
    left_ok = flags_ref[0] > 0
    right_ok = flags_ref[1] > 0
    rows = q_ref.shape[0]
    far_count = glob_ref.shape[1] + rand_ref.shape[1]
    keys = (3 + far_count) * BLK
    col = lax.broadcasted_iota(jnp.int32, (rows, keys), 1)
    bad = ((col < BLK) & jnp.logical_not(left_ok)) | (
        (col >= 2 * BLK) & (col < 3 * BLK) & jnp.logical_not(right_ok)
    )
    for g in range(q_ref.shape[1] // HEAD_DIM):
        sl = pl.ds(g * HEAD_DIM, HEAD_DIM)
        qh = q_ref[:, sl]
        k_all = jnp.concatenate(
            (
                left_ref[0, :, sl],
                own_ref[0, :, sl],
                right_ref[0, :, sl],
                *[glob_ref[0, j, 0, :, sl] for j in range(glob_ref.shape[1])],
                *[rand_ref[0, j, 0, :, sl] for j in range(rand_ref.shape[1])],
            ),
            axis=0,
        )
        scores = (
            lax.dot_general(
                qh, k_all, (((1,), (1,)), ((), ())), preferred_element_type=jnp.float32
            )
            * factor
        )
        scores = jnp.where(bad, neg_big, scores)
        highest = jnp.max(scores, axis=-1, keepdims=True)
        weights = jnp.exp(scores - highest)
        denominator = jnp.sum(weights, axis=-1, keepdims=True)
        v_all = jnp.concatenate(
            (
                left_ref[1, :, sl],
                own_ref[1, :, sl],
                right_ref[1, :, sl],
                *[glob_ref[0, j, 1, :, sl] for j in range(glob_ref.shape[1])],
                *[rand_ref[0, j, 1, :, sl] for j in range(rand_ref.shape[1])],
            ),
            axis=0,
        )
        mixed = jnp.dot(weights.astype(jnp.bfloat16), v_all, preferred_element_type=jnp.float32)
        o_ref[:, sl] = (mixed / denominator).astype(o_ref.dtype)


def far_spec(far, gw):
    per = far.shape[4] // gw
    return pl.BlockSpec(
        (1, far.shape[1], 2, BLK, gw), lambda h, f: (h // per, 0, 0, 0, h % per)
    )


def attend(flags, queries, own, left, right, glob, rand, gw):
    rows, width = queries.shape
    steps = width // gw
    kernel = functools.partial(attend_kernel, factor=1.0 / math.sqrt(HEAD_DIM))
    kv_spec = pl.BlockSpec((2, rows, gw), lambda h, f: (0, 0, h))
    return pl.pallas_call(
        kernel,
        out_shape=jax.ShapeDtypeStruct((rows, width), queries.dtype),
        grid_spec=pltpu.PrefetchScalarGridSpec(
            num_scalar_prefetch=1,
            grid=(steps,),
            in_specs=[
                pl.BlockSpec((rows, gw), lambda h, f: (0, h)),
                kv_spec,
                kv_spec,
                kv_spec,
                far_spec(glob, gw),
                far_spec(rand, gw),
            ],
            out_specs=pl.BlockSpec((rows, gw), lambda h, f: (0, h)),
        ),
    )(flags, queries, own, left, right, glob, rand)


def feature_major(far):
    peers, count, two, rows, piece = far.shape
    return far.transpose(1, 2, 3, 0, 4).reshape(1, count, two, rows, peers * piece)


def per_device(queries, key_rows, values, random_ids, global_ids):
    tok_rows, feat_width = queries.shape
    halves = lax.axis_size("half")
    sub = lax.axis_size("sub")
    peers = halves * sub
    seq = ("half", "sub")
    my_half = lax.axis_index("half")
    my_rank = my_half * sub + lax.axis_index("sub")
    local_blocks = tok_rows // BLK
    assert local_blocks == 1
    piece = feat_width // sub
    keyvals = jnp.stack((key_rows, values))
    pair = lax.all_gather(keyvals, "half", axis=0, tiled=False)
    pieces = pair.reshape(halves, 2, BLK, sub, piece).transpose(3, 0, 1, 2, 4)
    spread = lax.all_to_all(pieces, "sub", split_axis=0, concat_axis=0, tiled=True)
    spread = spread.reshape(sub * halves, 2, BLK, piece)

    def slot(block):
        return (block % sub) * halves + block // sub

    glob_piece = jnp.take(spread, slot(global_ids), axis=0, mode="clip")
    glob = lax.all_gather(glob_piece[None], "sub", axis=0, tiled=True)
    mine = lax.dynamic_slice_in_dim(random_ids, my_half * sub, sub, axis=0)
    outgoing = jnp.take(spread, slot(mine.reshape(-1)), axis=0, mode="clip")
    outgoing = outgoing.reshape(sub, RAND, 2, BLK, piece)
    rand = lax.all_to_all(outgoing, "sub", split_axis=0, concat_axis=0, tiled=True)
    left = shifted(keyvals, seq, 1, peers)
    right = shifted(keyvals, seq, -1, peers)
    flags = jnp.stack((my_rank > 0, my_rank < peers - 1)).astype(jnp.int32)
    if piece % HEAD_DIM == 0:
        gw = piece
    else:
        glob = feature_major(glob)
        rand = feature_major(rand)
        gw = GROUP * HEAD_DIM
    return attend(flags, queries, keyvals, left, right, glob, rand, gw)


def solution(mesh):
    groups, peers = mesh.devices.shape
    halves = 2 if peers % 2 == 0 else 1
    split = Mesh(mesh.devices.reshape(groups, halves, peers // halves), ("grp", "half", "sub"))
    rows = P(("grp", "half", "sub"), None)
    return jax.shard_map(
        per_device,
        mesh=split,
        in_specs=(rows, rows, rows, P("grp", None), P("grp")),
        out_specs=rows,
        check_vma=False,
    )
```

```python
import functools
import math

import jax
import jax.numpy as jnp
from jax import lax
from jax.experimental import pallas as pl
from jax.experimental.pallas import tpu as pltpu
from jax.sharding import PartitionSpec as P

HEADS = 32
HEAD_DIM = 128
BLK = 128
RAND = 3
GLOBAL = 2
GROUP = 4

neg_big = -1e30


def shifted(block, axis, step):
    count = lax.axis_size(axis)
    if step > 0:
        pairs = [(i, i + 1) for i in range(count - 1)]
    else:
        pairs = [(i + 1, i) for i in range(count - 1)]
    return lax.ppermute(block, axis, pairs)


def attend_kernel(
    flags_ref, q_ref, own_ref, left_ref, right_ref, glob_ref, rand_ref, o_ref, *, factor
):
    left_ok = flags_ref[0] > 0
    right_ok = flags_ref[1] > 0
    rows = q_ref.shape[0]
    far_count = glob_ref.shape[1] + rand_ref.shape[1]
    keys = (3 + far_count) * BLK
    col = lax.broadcasted_iota(jnp.int32, (rows, keys), 1)
    bad = ((col < BLK) & jnp.logical_not(left_ok)) | (
        (col >= 2 * BLK) & (col < 3 * BLK) & jnp.logical_not(right_ok)
    )
    piece_w = glob_ref.shape[4]
    for g in range(q_ref.shape[1] // HEAD_DIM):
        sl = pl.ds(g * HEAD_DIM, HEAD_DIM)
        src = (g * HEAD_DIM) // piece_w
        fsl = pl.ds((g * HEAD_DIM) % piece_w, HEAD_DIM)
        qh = q_ref[:, sl]
        k_all = jnp.concatenate(
            (
                left_ref[0, :, sl],
                own_ref[0, :, sl],
                right_ref[0, :, sl],
                *[glob_ref[src, j, 0, :, fsl] for j in range(glob_ref.shape[1])],
                *[rand_ref[src, j, 0, :, fsl] for j in range(rand_ref.shape[1])],
            ),
            axis=0,
        )
        scores = (
            lax.dot_general(
                qh, k_all, (((1,), (1,)), ((), ())), preferred_element_type=jnp.float32
            )
            * factor
        )
        scores = jnp.where(bad, neg_big, scores)
        highest = jnp.max(scores, axis=-1, keepdims=True)
        weights = jnp.exp(scores - highest)
        denominator = jnp.sum(weights, axis=-1, keepdims=True)
        v_all = jnp.concatenate(
            (
                left_ref[1, :, sl],
                own_ref[1, :, sl],
                right_ref[1, :, sl],
                *[glob_ref[src, j, 1, :, fsl] for j in range(glob_ref.shape[1])],
                *[rand_ref[src, j, 1, :, fsl] for j in range(rand_ref.shape[1])],
            ),
            axis=0,
        )
        mixed = jnp.dot(weights.astype(jnp.bfloat16), v_all, preferred_element_type=jnp.float32)
        o_ref[:, sl] = (mixed / denominator).astype(o_ref.dtype)


def far_spec(far, gw):
    width = far.shape[4]
    if width >= gw:
        per = width // gw
        return pl.BlockSpec(
            (1, far.shape[1], 2, BLK, gw), lambda h, f: (h // per, 0, 0, 0, h % per)
        )
    return pl.BlockSpec(
        (gw // width, far.shape[1], 2, BLK, width), lambda h, f: (h, 0, 0, 0, 0)
    )


def attend(flags, queries, own, left, right, glob, rand, gw):
    rows, width = queries.shape
    steps = width // gw
    kernel = functools.partial(attend_kernel, factor=1.0 / math.sqrt(HEAD_DIM))
    kv_spec = pl.BlockSpec((2, rows, gw), lambda h, f: (0, 0, h))
    return pl.pallas_call(
        kernel,
        out_shape=jax.ShapeDtypeStruct((rows, width), queries.dtype),
        grid_spec=pltpu.PrefetchScalarGridSpec(
            num_scalar_prefetch=1,
            grid=(steps,),
            in_specs=[
                pl.BlockSpec((rows, gw), lambda h, f: (0, h)),
                kv_spec,
                kv_spec,
                kv_spec,
                far_spec(glob, gw),
                far_spec(rand, gw),
            ],
            out_specs=pl.BlockSpec((rows, gw), lambda h, f: (0, h)),
        ),
    )(flags, queries, own, left, right, glob, rand)


def feature_major(far):
    peers, count, two, rows, piece = far.shape
    return far.transpose(1, 2, 3, 0, 4).reshape(1, count, two, rows, peers * piece)


def per_device(queries, key_rows, values, random_ids, global_ids):
    tok_rows, feat_width = queries.shape
    peers = lax.axis_size("seq")
    my_rank = lax.axis_index("seq")
    local_blocks = tok_rows // BLK
    assert local_blocks == 1
    all_blocks = local_blocks * peers
    piece = feat_width // peers
    keyvals = jnp.stack((key_rows, values))
    pieces = keyvals.reshape(2, BLK, peers, piece).transpose(2, 0, 1, 3)
    spread = lax.all_to_all(pieces, "seq", split_axis=0, concat_axis=0, tiled=True)
    glob_piece = jnp.take(spread, global_ids, axis=0, mode="clip")
    glob = lax.all_gather(glob_piece[None], "seq", axis=0, tiled=True)
    outgoing = jnp.take(spread, random_ids.reshape(-1), axis=0, mode="clip")
    outgoing = outgoing.reshape(all_blocks, RAND, 2, BLK, piece)
    left = shifted(keyvals, "seq", 1)
    right = shifted(keyvals, "seq", -1)
    outgoing, left, right = lax.optimization_barrier((outgoing, left, right))
    rand = lax.all_to_all(outgoing, "seq", split_axis=0, concat_axis=0, tiled=True)
    flags = jnp.stack((my_rank > 0, my_rank < peers - 1)).astype(jnp.int32)
    if piece % HEAD_DIM == 0:
        gw = GROUP * HEAD_DIM if (GROUP * HEAD_DIM) % piece == 0 else piece
    else:
        glob = feature_major(glob)
        rand = feature_major(rand)
        gw = GROUP * HEAD_DIM
    return attend(flags, queries, keyvals, left, right, glob, rand, gw)


def solution(mesh):
    return jax.shard_map(
        per_device,
        mesh=mesh,
        in_specs=(
            P(("grp", "seq"), None),
            P(("grp", "seq"), None),
            P(("grp", "seq"), None),
            P("grp", None),
            P("grp"),
        ),
        out_specs=P(("grp", "seq"), None),
        check_vma=False,
    )
```

```python
import functools
import math

import jax
import jax.numpy as jnp
from jax import lax
from jax.experimental import pallas as pl
from jax.experimental.pallas import tpu as pltpu
from jax.sharding import PartitionSpec as P

HEADS = 32
HEAD_DIM = 128
BLK = 128
RAND = 3
GLOBAL = 2
GROUP = 4

neg_big = -1e30


def shifted(block, axis, step):
    count = lax.axis_size(axis)
    if step > 0:
        pairs = [(i, i + 1) for i in range(count - 1)]
    else:
        pairs = [(i + 1, i) for i in range(count - 1)]
    return lax.ppermute(block, axis, pairs)


def attend_kernel(
    flags_ref, q_ref, own_ref, left_ref, right_ref, glob_ref, rand_ref, o_ref, *, factor
):
    left_ok = flags_ref[0] > 0
    right_ok = flags_ref[1] > 0
    rows = q_ref.shape[0]
    far_count = glob_ref.shape[1] + rand_ref.shape[1]
    keys = (3 + far_count) * BLK
    col = lax.broadcasted_iota(jnp.int32, (rows, keys), 1)
    bad = ((col < BLK) & jnp.logical_not(left_ok)) | (
        (col >= 2 * BLK) & (col < 3 * BLK) & jnp.logical_not(right_ok)
    )
    piece_w = glob_ref.shape[4]
    for g in range(q_ref.shape[1] // HEAD_DIM):
        sl = pl.ds(g * HEAD_DIM, HEAD_DIM)
        src = (g * HEAD_DIM) // piece_w
        fsl = pl.ds((g * HEAD_DIM) % piece_w, HEAD_DIM)
        qh = q_ref[:, sl]
        k_all = jnp.concatenate(
            (
                left_ref[src, 0, 0, :, fsl],
                own_ref[src, 0, 0, :, fsl],
                right_ref[src, 0, 0, :, fsl],
                *[glob_ref[src, j, 0, :, fsl] for j in range(glob_ref.shape[1])],
                *[rand_ref[src, j, 0, :, fsl] for j in range(rand_ref.shape[1])],
            ),
            axis=0,
        )
        scores = (
            lax.dot_general(
                qh, k_all, (((1,), (1,)), ((), ())), preferred_element_type=jnp.float32
            )
            * factor
        )
        scores = jnp.where(bad, neg_big, scores)
        highest = jnp.max(scores, axis=-1, keepdims=True)
        weights = jnp.exp(scores - highest)
        denominator = jnp.sum(weights, axis=-1, keepdims=True)
        v_all = jnp.concatenate(
            (
                left_ref[src, 0, 1, :, fsl],
                own_ref[src, 0, 1, :, fsl],
                right_ref[src, 0, 1, :, fsl],
                *[glob_ref[src, j, 1, :, fsl] for j in range(glob_ref.shape[1])],
                *[rand_ref[src, j, 1, :, fsl] for j in range(rand_ref.shape[1])],
            ),
            axis=0,
        )
        mixed = jnp.dot(weights.astype(jnp.bfloat16), v_all, preferred_element_type=jnp.float32)
        o_ref[:, sl] = (mixed / denominator).astype(o_ref.dtype)


def far_spec(far, gw):
    width = far.shape[4]
    if width >= gw:
        per = width // gw
        return pl.BlockSpec(
            (1, far.shape[1], 2, BLK, gw), lambda h, f: (h // per, 0, 0, 0, h % per)
        )
    return pl.BlockSpec(
        (gw // width, far.shape[1], 2, BLK, width), lambda h, f: (h, 0, 0, 0, 0)
    )


def attend(flags, queries, own, left, right, glob, rand, gw):
    rows, width = queries.shape
    steps = width // gw
    kernel = functools.partial(attend_kernel, factor=1.0 / math.sqrt(HEAD_DIM))
    return pl.pallas_call(
        kernel,
        out_shape=jax.ShapeDtypeStruct((rows, width), queries.dtype),
        grid_spec=pltpu.PrefetchScalarGridSpec(
            num_scalar_prefetch=1,
            grid=(steps,),
            in_specs=[
                pl.BlockSpec((rows, gw), lambda h, f: (0, h)),
                far_spec(own, gw),
                far_spec(left, gw),
                far_spec(right, gw),
                far_spec(glob, gw),
                far_spec(rand, gw),
            ],
            out_specs=pl.BlockSpec((rows, gw), lambda h, f: (0, h)),
        ),
    )(flags, queries, own, left, right, glob, rand)


def split_kernel(k_ref, v_ref, o_ref):
    o_ref[0, 0, 0] = k_ref[...]
    o_ref[0, 0, 1] = v_ref[...]


def split_pieces(key_rows, values, peers):
    rows, width = key_rows.shape
    piece = width // peers
    if piece % HEAD_DIM:
        keyvals = jnp.stack((key_rows, values))
        return keyvals.reshape(2, rows, peers, piece).transpose(2, 0, 1, 3)[:, None]
    return pl.pallas_call(
        split_kernel,
        out_shape=jax.ShapeDtypeStruct((peers, 1, 2, rows, piece), key_rows.dtype),
        grid=(peers,),
        in_specs=[
            pl.BlockSpec((rows, piece), lambda j: (0, j)),
            pl.BlockSpec((rows, piece), lambda j: (0, j)),
        ],
        out_specs=pl.BlockSpec((1, 1, 2, rows, piece), lambda j: (j, 0, 0, 0, 0)),
    )(key_rows, values)


def feature_major(far):
    peers, count, two, rows, piece = far.shape
    return far.transpose(1, 2, 3, 0, 4).reshape(1, count, two, rows, peers * piece)


def per_device(queries, key_rows, values, random_ids, global_ids):
    tok_rows, feat_width = queries.shape
    peers = lax.axis_size("seq")
    my_rank = lax.axis_index("seq")
    local_blocks = tok_rows // BLK
    assert local_blocks == 1
    all_blocks = local_blocks * peers
    piece = feat_width // peers
    pieces = split_pieces(key_rows, values, peers)
    spread = lax.all_to_all(pieces, "seq", split_axis=0, concat_axis=0, tiled=True)
    spread = spread.reshape(all_blocks, 2, BLK, piece)
    outgoing = jnp.take(spread, random_ids.reshape(-1), axis=0, mode="clip")
    outgoing = outgoing.reshape(all_blocks, RAND, 2, BLK, piece)
    left = shifted(pieces, "seq", 1)
    right = shifted(pieces, "seq", -1)
    outgoing, left, right = lax.optimization_barrier((outgoing, left, right))
    rand = lax.all_to_all(outgoing, "seq", split_axis=0, concat_axis=0, tiled=True)
    glob_piece = jnp.take(spread, global_ids, axis=0, mode="clip")
    glob = lax.all_gather(glob_piece[None], "seq", axis=0, tiled=True)
    flags = jnp.stack((my_rank > 0, my_rank < peers - 1)).astype(jnp.int32)
    if piece % HEAD_DIM == 0:
        gw = GROUP * HEAD_DIM if (GROUP * HEAD_DIM) % piece == 0 else piece
    else:
        glob = feature_major(glob)
        rand = feature_major(rand)
        gw = GROUP * HEAD_DIM
    own = pieces
    if piece % HEAD_DIM:
        own = feature_major(own)
        left = feature_major(left)
        right = feature_major(right)
    return attend(flags, queries, own, left, right, glob, rand, gw)


def solution(mesh):
    return jax.shard_map(
        per_device,
        mesh=mesh,
        in_specs=(
            P(("grp", "seq"), None),
            P(("grp", "seq"), None),
            P(("grp", "seq"), None),
            P("grp", None),
            P("grp"),
        ),
        out_specs=P(("grp", "seq"), None),
        check_vma=False,
    )
```

```python
import functools
import math

import jax
import jax.numpy as jnp
from jax import lax
from jax.experimental import pallas as pl
from jax.experimental.pallas import tpu as pltpu
from jax.sharding import PartitionSpec as P

HEADS = 32
HEAD_DIM = 128
BLK = 128
RAND = 3
GLOBAL = 2
GROUP = 4
SPLIT_WIDTH = 1024

neg_big = -1e30


def shifted(block, axis, step):
    count = lax.axis_size(axis)
    if step > 0:
        pairs = [(i, i + 1) for i in range(count - 1)]
    else:
        pairs = [(i + 1, i) for i in range(count - 1)]
    return lax.ppermute(block, axis, pairs)


def attend_kernel(
    flags_ref, q_ref, own_ref, left_ref, right_ref, glob_ref, rand_ref, o_ref, *, factor
):
    left_ok = flags_ref[0] > 0
    right_ok = flags_ref[1] > 0
    rows = q_ref.shape[0]
    far_count = glob_ref.shape[1] + rand_ref.shape[1]
    keys = (3 + far_count) * BLK
    col = lax.broadcasted_iota(jnp.int32, (rows, keys), 1)
    bad = ((col < BLK) & jnp.logical_not(left_ok)) | (
        (col >= 2 * BLK) & (col < 3 * BLK) & jnp.logical_not(right_ok)
    )
    piece_w = glob_ref.shape[4]
    for g in range(q_ref.shape[1] // HEAD_DIM):
        sl = pl.ds(g * HEAD_DIM, HEAD_DIM)
        src = (g * HEAD_DIM) // piece_w
        fsl = pl.ds((g * HEAD_DIM) % piece_w, HEAD_DIM)
        qh = q_ref[:, sl]
        k_all = jnp.concatenate(
            (
                left_ref[src, 0, 0, :, fsl],
                own_ref[src, 0, 0, :, fsl],
                right_ref[src, 0, 0, :, fsl],
                *[glob_ref[src, j, 0, :, fsl] for j in range(glob_ref.shape[1])],
                *[rand_ref[src, j, 0, :, fsl] for j in range(rand_ref.shape[1])],
            ),
            axis=0,
        )
        scores = (
            lax.dot_general(
                qh, k_all, (((1,), (1,)), ((), ())), preferred_element_type=jnp.float32
            )
            * factor
        )
        scores = jnp.where(bad, neg_big, scores)
        highest = jnp.max(scores, axis=-1, keepdims=True)
        weights = jnp.exp(scores - highest)
        denominator = jnp.sum(weights, axis=-1, keepdims=True)
        v_all = jnp.concatenate(
            (
                left_ref[src, 0, 1, :, fsl],
                own_ref[src, 0, 1, :, fsl],
                right_ref[src, 0, 1, :, fsl],
                *[glob_ref[src, j, 1, :, fsl] for j in range(glob_ref.shape[1])],
                *[rand_ref[src, j, 1, :, fsl] for j in range(rand_ref.shape[1])],
            ),
            axis=0,
        )
        mixed = jnp.dot(weights.astype(jnp.bfloat16), v_all, preferred_element_type=jnp.float32)
        o_ref[:, sl] = (mixed / denominator).astype(o_ref.dtype)


def far_spec(far, gw):
    width = far.shape[4]
    if width >= gw:
        per = width // gw
        return pl.BlockSpec(
            (1, far.shape[1], 2, BLK, gw), lambda h, f: (h // per, 0, 0, 0, h % per)
        )
    return pl.BlockSpec(
        (gw // width, far.shape[1], 2, BLK, width), lambda h, f: (h, 0, 0, 0, 0)
    )


def attend(flags, queries, own, left, right, glob, rand, gw):
    rows, width = queries.shape
    steps = width // gw
    kernel = functools.partial(attend_kernel, factor=1.0 / math.sqrt(HEAD_DIM))
    return pl.pallas_call(
        kernel,
        out_shape=jax.ShapeDtypeStruct((rows, width), queries.dtype),
        grid_spec=pltpu.PrefetchScalarGridSpec(
            num_scalar_prefetch=1,
            grid=(steps,),
            in_specs=[
                pl.BlockSpec((rows, gw), lambda h, f: (0, h)),
                far_spec(own, gw),
                far_spec(left, gw),
                far_spec(right, gw),
                far_spec(glob, gw),
                far_spec(rand, gw),
            ],
            out_specs=pl.BlockSpec((rows, gw), lambda h, f: (0, h)),
        ),
    )(flags, queries, own, left, right, glob, rand)


def split_kernel(k_ref, v_ref, o_ref):
    piece = o_ref.shape[4]
    for j in range(o_ref.shape[0]):
        o_ref[j, 0, 0] = k_ref[:, pl.ds(j * piece, piece)]
        o_ref[j, 0, 1] = v_ref[:, pl.ds(j * piece, piece)]


def split_pieces(key_rows, values, peers):
    rows, width = key_rows.shape
    piece = width // peers
    if piece % HEAD_DIM:
        keyvals = jnp.stack((key_rows, values))
        return keyvals.reshape(2, rows, peers, piece).transpose(2, 0, 1, 3)[:, None]
    per = max(1, min(peers, SPLIT_WIDTH // piece))
    while peers % per:
        per -= 1
    return pl.pallas_call(
        split_kernel,
        out_shape=jax.ShapeDtypeStruct((peers, 1, 2, rows, piece), key_rows.dtype),
        grid=(peers // per,),
        in_specs=[
            pl.BlockSpec((rows, per * piece), lambda j: (0, j)),
            pl.BlockSpec((rows, per * piece), lambda j: (0, j)),
        ],
        out_specs=pl.BlockSpec((per, 1, 2, rows, piece), lambda j: (j, 0, 0, 0, 0)),
    )(key_rows, values)


def feature_major(far):
    peers, count, two, rows, piece = far.shape
    return far.transpose(1, 2, 3, 0, 4).reshape(1, count, two, rows, peers * piece)


def per_device(queries, key_rows, values, random_ids, global_ids):
    tok_rows, feat_width = queries.shape
    peers = lax.axis_size("seq")
    my_rank = lax.axis_index("seq")
    local_blocks = tok_rows // BLK
    assert local_blocks == 1
    all_blocks = local_blocks * peers
    piece = feat_width // peers
    pieces = split_pieces(key_rows, values, peers)
    spread = lax.all_to_all(pieces, "seq", split_axis=0, concat_axis=0, tiled=True)
    spread = spread.reshape(all_blocks, 2, BLK, piece)
    outgoing = jnp.take(spread, random_ids.reshape(-1), axis=0, mode="clip")
    outgoing = outgoing.reshape(all_blocks, RAND, 2, BLK, piece)
    left = shifted(pieces, "seq", 1)
    right = shifted(pieces, "seq", -1)
    outgoing, left, right = lax.optimization_barrier((outgoing, left, right))
    rand = lax.all_to_all(outgoing, "seq", split_axis=0, concat_axis=0, tiled=True)
    glob_piece = jnp.take(spread, global_ids, axis=0, mode="clip")
    glob = lax.all_gather(glob_piece[None], "seq", axis=0, tiled=True)
    flags = jnp.stack((my_rank > 0, my_rank < peers - 1)).astype(jnp.int32)
    if piece % HEAD_DIM == 0:
        gw = GROUP * HEAD_DIM if (GROUP * HEAD_DIM) % piece == 0 else piece
    else:
        glob = feature_major(glob)
        rand = feature_major(rand)
        gw = GROUP * HEAD_DIM
    own = pieces
    if piece % HEAD_DIM:
        own = feature_major(own)
        left = feature_major(left)
        right = feature_major(right)
    return attend(flags, queries, own, left, right, glob, rand, gw)


def solution(mesh):
    return jax.shard_map(
        per_device,
        mesh=mesh,
        in_specs=(
            P(("grp", "seq"), None),
            P(("grp", "seq"), None),
            P(("grp", "seq"), None),
            P("grp", None),
            P("grp"),
        ),
        out_specs=P(("grp", "seq"), None),
        check_vma=False,
    )
```

```python
import functools
import math

import jax
import jax.numpy as jnp
from jax import lax
from jax.experimental import pallas as pl
from jax.experimental.pallas import tpu as pltpu
from jax.sharding import PartitionSpec as P

HEADS = 32
HEAD_DIM = 128
BLK = 128
RAND = 3
GLOBAL = 2
GROUP = 4
SPLIT_WIDTH = 1024
HALVES = 2

neg_big = -1e30


def shifted(block, axis, step):
    count = lax.axis_size(axis)
    if step > 0:
        pairs = [(i, i + 1) for i in range(count - 1)]
    else:
        pairs = [(i + 1, i) for i in range(count - 1)]
    return lax.ppermute(block, axis, pairs)


def attend_kernel(
    flags_ref, q_ref, own_ref, left_ref, right_ref, glob_ref, rand_ref, o_ref, *, factor
):
    left_ok = flags_ref[0] > 0
    right_ok = flags_ref[1] > 0
    rows = q_ref.shape[0]
    far_count = glob_ref.shape[1] + rand_ref.shape[1]
    keys = (3 + far_count) * BLK
    col = lax.broadcasted_iota(jnp.int32, (rows, keys), 1)
    bad = ((col < BLK) & jnp.logical_not(left_ok)) | (
        (col >= 2 * BLK) & (col < 3 * BLK) & jnp.logical_not(right_ok)
    )
    piece_w = glob_ref.shape[4]
    for g in range(q_ref.shape[1] // HEAD_DIM):
        sl = pl.ds(g * HEAD_DIM, HEAD_DIM)
        src = (g * HEAD_DIM) // piece_w
        fsl = pl.ds((g * HEAD_DIM) % piece_w, HEAD_DIM)
        qh = q_ref[:, sl]
        k_all = jnp.concatenate(
            (
                left_ref[src, 0, 0, :, fsl],
                own_ref[src, 0, 0, :, fsl],
                right_ref[src, 0, 0, :, fsl],
                *[glob_ref[src, j, 0, :, fsl] for j in range(glob_ref.shape[1])],
                *[rand_ref[src, j, 0, :, fsl] for j in range(rand_ref.shape[1])],
            ),
            axis=0,
        )
        scores = (
            lax.dot_general(
                qh, k_all, (((1,), (1,)), ((), ())), preferred_element_type=jnp.float32
            )
            * factor
        )
        scores = jnp.where(bad, neg_big, scores)
        highest = jnp.max(scores, axis=-1, keepdims=True)
        weights = jnp.exp(scores - highest)
        denominator = jnp.sum(weights, axis=-1, keepdims=True)
        v_all = jnp.concatenate(
            (
                left_ref[src, 0, 1, :, fsl],
                own_ref[src, 0, 1, :, fsl],
                right_ref[src, 0, 1, :, fsl],
                *[glob_ref[src, j, 1, :, fsl] for j in range(glob_ref.shape[1])],
                *[rand_ref[src, j, 1, :, fsl] for j in range(rand_ref.shape[1])],
            ),
            axis=0,
        )
        mixed = jnp.dot(weights.astype(jnp.bfloat16), v_all, preferred_element_type=jnp.float32)
        o_ref[:, sl] = (mixed / denominator).astype(o_ref.dtype)


def far_spec(far, gw, sel=None):
    width = far.shape[4]
    count = far.shape[1] if sel is None else 1
    at = 0 if sel is None else sel
    if width >= gw:
        per = width // gw
        return pl.BlockSpec(
            (1, count, 2, BLK, gw), lambda h, f: (h // per, at, 0, 0, h % per)
        )
    return pl.BlockSpec(
        (gw // width, count, 2, BLK, width), lambda h, f: (h, at, 0, 0, 0)
    )


def attend(flags, queries, own, left, right, glob, rand, gw, half, halves):
    rows, width = queries.shape
    part = width // halves
    steps = part // gw
    kernel = functools.partial(attend_kernel, factor=1.0 / math.sqrt(HEAD_DIM))
    sel = half if own.shape[1] == halves and halves > 1 else None
    return pl.pallas_call(
        kernel,
        out_shape=jax.ShapeDtypeStruct((rows, part), queries.dtype),
        grid_spec=pltpu.PrefetchScalarGridSpec(
            num_scalar_prefetch=1,
            grid=(steps,),
            in_specs=[
                pl.BlockSpec((rows, gw), lambda h, f: (0, half * steps + h)),
                far_spec(own, gw, sel),
                far_spec(left, gw, sel),
                far_spec(right, gw, sel),
                far_spec(glob, gw),
                far_spec(rand, gw),
            ],
            out_specs=pl.BlockSpec((rows, gw), lambda h, f: (0, h)),
        ),
    )(flags, queries, own, left, right, glob, rand)


def split_kernel(k_ref, v_ref, o_ref):
    piece = o_ref.shape[4]
    for j in range(o_ref.shape[0]):
        o_ref[j, 0, 0] = k_ref[:, pl.ds(j * piece, piece)]
        o_ref[j, 0, 1] = v_ref[:, pl.ds(j * piece, piece)]


def split_pieces(key_rows, values, peers, halves):
    rows, width = key_rows.shape
    piece = width // (peers * halves)
    if halves == 1 and piece % HEAD_DIM:
        keyvals = jnp.stack((key_rows, values))
        return keyvals.reshape(2, rows, peers, piece).transpose(2, 0, 1, 3)[:, None]
    per = max(1, min(peers, SPLIT_WIDTH // piece))
    while peers % per:
        per -= 1
    chunks = peers // per
    return pl.pallas_call(
        split_kernel,
        out_shape=jax.ShapeDtypeStruct((peers, halves, 2, rows, piece), key_rows.dtype),
        grid=(halves, chunks),
        in_specs=[
            pl.BlockSpec((rows, per * piece), lambda a, j: (0, a * chunks + j)),
            pl.BlockSpec((rows, per * piece), lambda a, j: (0, a * chunks + j)),
        ],
        out_specs=pl.BlockSpec((per, 1, 2, rows, piece), lambda a, j: (j, a, 0, 0, 0)),
    )(key_rows, values)


def feature_major(far):
    peers, count, two, rows, piece = far.shape
    return far.transpose(1, 2, 3, 0, 4).reshape(1, count, two, rows, peers * piece)


def per_device(queries, key_rows, values, random_ids, global_ids):
    tok_rows, feat_width = queries.shape
    peers = lax.axis_size("seq")
    my_rank = lax.axis_index("seq")
    local_blocks = tok_rows // BLK
    assert local_blocks == 1
    all_blocks = local_blocks * peers
    halves = HALVES if (feat_width // (peers * HALVES)) % HEAD_DIM == 0 else 1
    piece = feat_width // (peers * halves)
    pieces = split_pieces(key_rows, values, peers, halves)
    spread = lax.all_to_all(pieces, "seq", split_axis=0, concat_axis=0, tiled=True)
    picked = jnp.take(spread, random_ids.reshape(-1), axis=0, mode="clip")
    outgoing = [
        picked[:, a].reshape(all_blocks, RAND, 2, BLK, piece) for a in range(halves)
    ]
    left = shifted(pieces, "seq", 1)
    right = shifted(pieces, "seq", -1)
    first, left, right = lax.optimization_barrier((outgoing[0], left, right))
    outgoing[0] = first
    glob_all = jnp.take(spread, global_ids, axis=0, mode="clip")
    flags = jnp.stack((my_rank > 0, my_rank < peers - 1)).astype(jnp.int32)
    if piece % HEAD_DIM == 0:
        gw = GROUP * HEAD_DIM if (GROUP * HEAD_DIM) % piece == 0 else piece
        own = pieces
    else:
        gw = GROUP * HEAD_DIM
        own = feature_major(pieces)
        left = feature_major(left)
        right = feature_major(right)
    outs = []
    for a in range(halves):
        rand = lax.all_to_all(outgoing[a], "seq", split_axis=0, concat_axis=0, tiled=True)
        glob = lax.all_gather(glob_all[None, :, a], "seq", axis=0, tiled=True)
        if piece % HEAD_DIM:
            rand = feature_major(rand)
            glob = feature_major(glob)
        outs.append(attend(flags, queries, own, left, right, glob, rand, gw, a, halves))
    return outs[0] if halves == 1 else jnp.concatenate(outs, axis=1)


def solution(mesh):
    return jax.shard_map(
        per_device,
        mesh=mesh,
        in_specs=(
            P(("grp", "seq"), None),
            P(("grp", "seq"), None),
            P(("grp", "seq"), None),
            P("grp", None),
            P("grp"),
        ),
        out_specs=P(("grp", "seq"), None),
        check_vma=False,
    )
```

```python
import functools
import math

import jax
import jax.numpy as jnp
from jax import lax
from jax.experimental import pallas as pl
from jax.experimental.pallas import tpu as pltpu
from jax.sharding import PartitionSpec as P

HEADS = 32
HEAD_DIM = 128
BLK = 128
RAND = 3
GLOBAL = 2
GROUP = 8
SPLIT_WIDTH = 1024

neg_big = -1e30


def shifted(block, axis, step):
    count = lax.axis_size(axis)
    if step > 0:
        pairs = [(i, i + 1) for i in range(count - 1)]
    else:
        pairs = [(i + 1, i) for i in range(count - 1)]
    return lax.ppermute(block, axis, pairs)


def attend_kernel(
    flags_ref, q_ref, own_ref, left_ref, right_ref, glob_ref, rand_ref, o_ref, *, factor
):
    left_ok = flags_ref[0] > 0
    right_ok = flags_ref[1] > 0
    rows = q_ref.shape[0]
    far_count = glob_ref.shape[1] + rand_ref.shape[1]
    keys = (3 + far_count) * BLK
    col = lax.broadcasted_iota(jnp.int32, (rows, keys), 1)
    bad = ((col < BLK) & jnp.logical_not(left_ok)) | (
        (col >= 2 * BLK) & (col < 3 * BLK) & jnp.logical_not(right_ok)
    )
    piece_w = glob_ref.shape[4]
    for g in range(q_ref.shape[1] // HEAD_DIM):
        sl = pl.ds(g * HEAD_DIM, HEAD_DIM)
        src = (g * HEAD_DIM) // piece_w
        fsl = pl.ds((g * HEAD_DIM) % piece_w, HEAD_DIM)
        qh = q_ref[:, sl]
        k_all = jnp.concatenate(
            (
                left_ref[src, 0, 0, :, fsl],
                own_ref[src, 0, 0, :, fsl],
                right_ref[src, 0, 0, :, fsl],
                *[glob_ref[src, j, 0, :, fsl] for j in range(glob_ref.shape[1])],
                *[rand_ref[src, j, 0, :, fsl] for j in range(rand_ref.shape[1])],
            ),
            axis=0,
        )
        scores = (
            lax.dot_general(
                qh, k_all, (((1,), (1,)), ((), ())), preferred_element_type=jnp.float32
            )
            * factor
        )
        scores = jnp.where(bad, neg_big, scores)
        highest = jnp.max(scores, axis=-1, keepdims=True)
        weights = jnp.exp(scores - highest)
        denominator = jnp.sum(weights, axis=-1, keepdims=True)
        v_all = jnp.concatenate(
            (
                left_ref[src, 0, 1, :, fsl],
                own_ref[src, 0, 1, :, fsl],
                right_ref[src, 0, 1, :, fsl],
                *[glob_ref[src, j, 1, :, fsl] for j in range(glob_ref.shape[1])],
                *[rand_ref[src, j, 1, :, fsl] for j in range(rand_ref.shape[1])],
            ),
            axis=0,
        )
        mixed = jnp.dot(weights.astype(jnp.bfloat16), v_all, preferred_element_type=jnp.float32)
        o_ref[:, sl] = (mixed / denominator).astype(o_ref.dtype)


def far_spec(far, gw):
    width = far.shape[4]
    if width >= gw:
        per = width // gw
        return pl.BlockSpec(
            (1, far.shape[1], 2, BLK, gw), lambda h, f: (h // per, 0, 0, 0, h % per)
        )
    return pl.BlockSpec(
        (gw // width, far.shape[1], 2, BLK, width), lambda h, f: (h, 0, 0, 0, 0)
    )


def attend(flags, queries, own, left, right, glob, rand, gw):
    rows, width = queries.shape
    steps = width // gw
    kernel = functools.partial(attend_kernel, factor=1.0 / math.sqrt(HEAD_DIM))
    return pl.pallas_call(
        kernel,
        out_shape=jax.ShapeDtypeStruct((rows, width), queries.dtype),
        grid_spec=pltpu.PrefetchScalarGridSpec(
            num_scalar_prefetch=1,
            grid=(steps,),
            in_specs=[
                pl.BlockSpec((rows, gw), lambda h, f: (0, h)),
                far_spec(own, gw),
                far_spec(left, gw),
                far_spec(right, gw),
                far_spec(glob, gw),
                far_spec(rand, gw),
            ],
            out_specs=pl.BlockSpec((rows, gw), lambda h, f: (0, h)),
        ),
    )(flags, queries, own, left, right, glob, rand)


def split_kernel(k_ref, v_ref, o_ref):
    piece = o_ref.shape[4]
    for j in range(o_ref.shape[0]):
        o_ref[j, 0, 0] = k_ref[:, pl.ds(j * piece, piece)]
        o_ref[j, 0, 1] = v_ref[:, pl.ds(j * piece, piece)]


def split_pieces(key_rows, values, peers):
    rows, width = key_rows.shape
    piece = width // peers
    if piece % HEAD_DIM:
        keyvals = jnp.stack((key_rows, values))
        return keyvals.reshape(2, rows, peers, piece).transpose(2, 0, 1, 3)[:, None]
    per = max(1, min(peers, SPLIT_WIDTH // piece))
    while peers % per:
        per -= 1
    return pl.pallas_call(
        split_kernel,
        out_shape=jax.ShapeDtypeStruct((peers, 1, 2, rows, piece), key_rows.dtype),
        grid=(peers // per,),
        in_specs=[
            pl.BlockSpec((rows, per * piece), lambda j: (0, j)),
            pl.BlockSpec((rows, per * piece), lambda j: (0, j)),
        ],
        out_specs=pl.BlockSpec((per, 1, 2, rows, piece), lambda j: (j, 0, 0, 0, 0)),
    )(key_rows, values)


def feature_major(far):
    peers, count, two, rows, piece = far.shape
    return far.transpose(1, 2, 3, 0, 4).reshape(1, count, two, rows, peers * piece)


def per_device(queries, key_rows, values, random_ids, global_ids):
    tok_rows, feat_width = queries.shape
    peers = lax.axis_size("seq")
    my_rank = lax.axis_index("seq")
    local_blocks = tok_rows // BLK
    assert local_blocks == 1
    all_blocks = local_blocks * peers
    piece = feat_width // peers
    pieces = split_pieces(key_rows, values, peers)
    spread = lax.all_to_all(pieces, "seq", split_axis=0, concat_axis=0, tiled=True)
    spread = spread.reshape(all_blocks, 2, BLK, piece)
    outgoing = jnp.take(spread, random_ids.reshape(-1), axis=0, mode="clip")
    outgoing = outgoing.reshape(all_blocks, RAND, 2, BLK, piece)
    left = shifted(pieces, "seq", 1)
    right = shifted(pieces, "seq", -1)
    outgoing, left, right = lax.optimization_barrier((outgoing, left, right))
    rand = lax.all_to_all(outgoing, "seq", split_axis=0, concat_axis=0, tiled=True)
    glob_piece = jnp.take(spread, global_ids, axis=0, mode="clip")
    glob = lax.all_gather(glob_piece[None], "seq", axis=0, tiled=True)
    flags = jnp.stack((my_rank > 0, my_rank < peers - 1)).astype(jnp.int32)
    if piece % HEAD_DIM == 0:
        gw = GROUP * HEAD_DIM if (GROUP * HEAD_DIM) % piece == 0 else piece
    else:
        glob = feature_major(glob)
        rand = feature_major(rand)
        gw = GROUP * HEAD_DIM
    own = pieces
    if piece % HEAD_DIM:
        own = feature_major(own)
        left = feature_major(left)
        right = feature_major(right)
    return attend(flags, queries, own, left, right, glob, rand, gw)


def solution(mesh):
    return jax.shard_map(
        per_device,
        mesh=mesh,
        in_specs=(
            P(("grp", "seq"), None),
            P(("grp", "seq"), None),
            P(("grp", "seq"), None),
            P("grp", None),
            P("grp"),
        ),
        out_specs=P(("grp", "seq"), None),
        check_vma=False,
    )
```

```python
import functools
import math

import jax
import jax.numpy as jnp
from jax import lax
from jax.experimental import pallas as pl
from jax.experimental.pallas import tpu as pltpu
from jax.sharding import Mesh, PartitionSpec as P

HEADS = 32
HEAD_DIM = 128
BLK = 128
RAND = 3
GLOBAL = 2
GROUP = 8
SPLIT_WIDTH = 1024

neg_big = -1e30


def shifted(block, axis, step, count):
    if step > 0:
        pairs = [(i, i + 1) for i in range(count - 1)]
    else:
        pairs = [(i + 1, i) for i in range(count - 1)]
    return lax.ppermute(block, axis, pairs)


def attend_kernel(
    flags_ref, q_ref, own_ref, left_ref, right_ref, glob_ref, rand_ref, o_ref, *, factor
):
    left_ok = flags_ref[0] > 0
    right_ok = flags_ref[1] > 0
    rows = q_ref.shape[0]
    far_count = glob_ref.shape[2] + rand_ref.shape[1]
    parity = glob_ref.shape[0]
    keys = (3 + far_count) * BLK
    col = lax.broadcasted_iota(jnp.int32, (rows, keys), 1)
    bad = ((col < BLK) & jnp.logical_not(left_ok)) | (
        (col >= 2 * BLK) & (col < 3 * BLK) & jnp.logical_not(right_ok)
    )
    piece_w = rand_ref.shape[4]
    for g in range(q_ref.shape[1] // HEAD_DIM):
        sl = pl.ds(g * HEAD_DIM, HEAD_DIM)
        src = (g * HEAD_DIM) // piece_w
        fsl = pl.ds((g * HEAD_DIM) % piece_w, HEAD_DIM)
        qh = q_ref[:, sl]
        k_all = jnp.concatenate(
            (
                left_ref[src, 0, 0, :, fsl],
                own_ref[src, 0, 0, :, fsl],
                right_ref[src, 0, 0, :, fsl],
                *[
                    glob_ref[src % parity, src // parity, j, 0, :, fsl]
                    for j in range(glob_ref.shape[2])
                ],
                *[rand_ref[src, j, 0, :, fsl] for j in range(rand_ref.shape[1])],
            ),
            axis=0,
        )
        scores = (
            lax.dot_general(
                qh, k_all, (((1,), (1,)), ((), ())), preferred_element_type=jnp.float32
            )
            * factor
        )
        scores = jnp.where(bad, neg_big, scores)
        highest = jnp.max(scores, axis=-1, keepdims=True)
        weights = jnp.exp(scores - highest)
        denominator = jnp.sum(weights, axis=-1, keepdims=True)
        v_all = jnp.concatenate(
            (
                left_ref[src, 0, 1, :, fsl],
                own_ref[src, 0, 1, :, fsl],
                right_ref[src, 0, 1, :, fsl],
                *[
                    glob_ref[src % parity, src // parity, j, 1, :, fsl]
                    for j in range(glob_ref.shape[2])
                ],
                *[rand_ref[src, j, 1, :, fsl] for j in range(rand_ref.shape[1])],
            ),
            axis=0,
        )
        mixed = jnp.dot(weights.astype(jnp.bfloat16), v_all, preferred_element_type=jnp.float32)
        o_ref[:, sl] = (mixed / denominator).astype(o_ref.dtype)


def far_spec(far, gw):
    width = far.shape[4]
    if width >= gw:
        per = width // gw
        return pl.BlockSpec(
            (1, far.shape[1], 2, BLK, gw), lambda h, f: (h // per, 0, 0, 0, h % per)
        )
    return pl.BlockSpec(
        (gw // width, far.shape[1], 2, BLK, width), lambda h, f: (h, 0, 0, 0, 0)
    )


def glob_spec(glob, gw):
    parity, chips, count, two, rows, width = glob.shape
    if width >= gw:
        per = width // gw
        return pl.BlockSpec(
            (1, 1, count, 2, BLK, gw),
            lambda h, f: ((h // per) % parity, (h // per) // parity, 0, 0, 0, h % per),
        )
    sps = gw // width
    return pl.BlockSpec(
        (parity, sps // parity, count, 2, BLK, width), lambda h, f: (0, h, 0, 0, 0, 0)
    )


def attend(flags, queries, own, left, right, glob, rand, gw):
    rows, width = queries.shape
    steps = width // gw
    kernel = functools.partial(attend_kernel, factor=1.0 / math.sqrt(HEAD_DIM))
    return pl.pallas_call(
        kernel,
        out_shape=jax.ShapeDtypeStruct((rows, width), queries.dtype),
        grid_spec=pltpu.PrefetchScalarGridSpec(
            num_scalar_prefetch=1,
            grid=(steps,),
            in_specs=[
                pl.BlockSpec((rows, gw), lambda h, f: (0, h)),
                far_spec(own, gw),
                far_spec(left, gw),
                far_spec(right, gw),
                glob_spec(glob, gw),
                far_spec(rand, gw),
            ],
            out_specs=pl.BlockSpec((rows, gw), lambda h, f: (0, h)),
        ),
    )(flags, queries, own, left, right, glob, rand)


def split_kernel(k_ref, v_ref, o_ref):
    piece = o_ref.shape[4]
    for j in range(o_ref.shape[0]):
        o_ref[j, 0, 0] = k_ref[:, pl.ds(j * piece, piece)]
        o_ref[j, 0, 1] = v_ref[:, pl.ds(j * piece, piece)]


def split_pieces(key_rows, values, peers):
    rows, width = key_rows.shape
    piece = width // peers
    if piece % HEAD_DIM:
        keyvals = jnp.stack((key_rows, values))
        return keyvals.reshape(2, rows, peers, piece).transpose(2, 0, 1, 3)[:, None]
    per = max(1, min(peers, SPLIT_WIDTH // piece))
    while peers % per:
        per -= 1
    return pl.pallas_call(
        split_kernel,
        out_shape=jax.ShapeDtypeStruct((peers, 1, 2, rows, piece), key_rows.dtype),
        grid=(peers // per,),
        in_specs=[
            pl.BlockSpec((rows, per * piece), lambda j: (0, j)),
            pl.BlockSpec((rows, per * piece), lambda j: (0, j)),
        ],
        out_specs=pl.BlockSpec((per, 1, 2, rows, piece), lambda j: (j, 0, 0, 0, 0)),
    )(key_rows, values)


def feature_major(far):
    peers, count, two, rows, piece = far.shape
    return far.transpose(1, 2, 3, 0, 4).reshape(1, count, two, rows, peers * piece)


def per_device(queries, key_rows, values, random_ids, global_ids):
    tok_rows, feat_width = queries.shape
    cores = lax.axis_size("core")
    peers = lax.axis_size("chip") * cores
    seq = ("chip", "core")
    my_rank = lax.axis_index("chip") * cores + lax.axis_index("core")
    local_blocks = tok_rows // BLK
    assert local_blocks == 1
    all_blocks = local_blocks * peers
    piece = feat_width // peers
    pieces = split_pieces(key_rows, values, peers)
    spread = lax.all_to_all(pieces, seq, split_axis=0, concat_axis=0, tiled=True)
    spread = spread.reshape(all_blocks, 2, BLK, piece)
    outgoing = jnp.take(spread, random_ids.reshape(-1), axis=0, mode="clip")
    outgoing = outgoing.reshape(all_blocks, RAND, 2, BLK, piece)
    left = shifted(pieces, seq, 1, peers)
    right = shifted(pieces, seq, -1, peers)
    outgoing, left, right = lax.optimization_barrier((outgoing, left, right))
    rand = lax.all_to_all(outgoing, seq, split_axis=0, concat_axis=0, tiled=True)
    glob_piece = jnp.take(spread, global_ids, axis=0, mode="clip")
    glob = lax.all_gather(glob_piece[None], "chip", axis=0, tiled=True)
    glob = lax.all_gather(glob, "core", axis=0, tiled=False)
    flags = jnp.stack((my_rank > 0, my_rank < peers - 1)).astype(jnp.int32)
    if piece % HEAD_DIM == 0:
        gw = GROUP * HEAD_DIM if (GROUP * HEAD_DIM) % piece == 0 else piece
        own = pieces
    else:
        gw = GROUP * HEAD_DIM
        flat = glob.transpose(1, 0, 2, 3, 4, 5).reshape((peers,) + glob.shape[2:])
        glob = feature_major(flat)[None]
        rand = feature_major(rand)
        own = feature_major(pieces)
        left = feature_major(left)
        right = feature_major(right)
    return attend(flags, queries, own, left, right, glob, rand, gw)


def solution(mesh):
    groups, peers = mesh.devices.shape
    split = Mesh(mesh.devices.reshape(groups, peers // 2, 2), ("grp", "chip", "core"))
    rows = P(("grp", "chip", "core"), None)
    return jax.shard_map(
        per_device,
        mesh=split,
        in_specs=(rows, rows, rows, P("grp", None), P("grp")),
        out_specs=rows,
        check_vma=False,
    )
```

```python
import functools
import math

import jax
import jax.numpy as jnp
from jax import lax
from jax.experimental import pallas as pl
from jax.experimental.pallas import tpu as pltpu
from jax.sharding import PartitionSpec as P

HEADS = 32
HEAD_DIM = 128
BLK = 128
RAND = 3
GLOBAL = 2
GROUP = 8
SPLIT_WIDTH = 1024

neg_big = -1e30


def shifted(block, axis, step):
    count = lax.axis_size(axis)
    if step > 0:
        pairs = [(i, i + 1) for i in range(count - 1)]
    else:
        pairs = [(i + 1, i) for i in range(count - 1)]
    return lax.ppermute(block, axis, pairs)


def attend_kernel(
    flags_ref, q_ref, own_ref, left_ref, right_ref, glob_ref, rand_ref, o_ref, *, factor
):
    left_ok = flags_ref[0] > 0
    right_ok = flags_ref[1] > 0
    piece_w = glob_ref.shape[4]
    for g in range(q_ref.shape[1] // HEAD_DIM):
        sl = pl.ds(g * HEAD_DIM, HEAD_DIM)
        src = (g * HEAD_DIM) // piece_w
        fsl = pl.ds((g * HEAD_DIM) % piece_w, HEAD_DIM)
        qh = q_ref[:, sl]
        blocks = [
            (left_ref, 0),
            (own_ref, 0),
            (right_ref, 0),
            *[(glob_ref, j) for j in range(glob_ref.shape[1])],
            *[(rand_ref, j) for j in range(rand_ref.shape[1])],
        ]
        scores = []
        for ref, j in blocks:
            part = lax.dot_general(
                qh, ref[src, j, 0, :, fsl], (((1,), (1,)), ((), ())),
                preferred_element_type=jnp.float32,
            ) * factor
            scores.append(part)
        scores[0] = jnp.where(left_ok, scores[0], neg_big)
        scores[2] = jnp.where(right_ok, scores[2], neg_big)
        highest = functools.reduce(jnp.maximum, scores).max(axis=-1, keepdims=True)
        denominator = None
        mixed = None
        for (ref, j), part in zip(blocks, scores):
            weights = jnp.exp(part - highest)
            total = jnp.sum(weights, axis=-1, keepdims=True)
            term = jnp.dot(
                weights.astype(jnp.bfloat16), ref[src, j, 1, :, fsl],
                preferred_element_type=jnp.float32,
            )
            denominator = total if denominator is None else denominator + total
            mixed = term if mixed is None else mixed + term
        o_ref[:, sl] = (mixed / denominator).astype(o_ref.dtype)


def far_spec(far, gw):
    width = far.shape[4]
    if width >= gw:
        per = width // gw
        return pl.BlockSpec(
            (1, far.shape[1], 2, BLK, gw), lambda h, f: (h // per, 0, 0, 0, h % per)
        )
    return pl.BlockSpec(
        (gw // width, far.shape[1], 2, BLK, width), lambda h, f: (h, 0, 0, 0, 0)
    )


def attend(flags, queries, own, left, right, glob, rand, gw):
    rows, width = queries.shape
    steps = width // gw
    kernel = functools.partial(attend_kernel, factor=1.0 / math.sqrt(HEAD_DIM))
    return pl.pallas_call(
        kernel,
        out_shape=jax.ShapeDtypeStruct((rows, width), queries.dtype),
        grid_spec=pltpu.PrefetchScalarGridSpec(
            num_scalar_prefetch=1,
            grid=(steps,),
            in_specs=[
                pl.BlockSpec((rows, gw), lambda h, f: (0, h)),
                far_spec(own, gw),
                far_spec(left, gw),
                far_spec(right, gw),
                far_spec(glob, gw),
                far_spec(rand, gw),
            ],
            out_specs=pl.BlockSpec((rows, gw), lambda h, f: (0, h)),
        ),
    )(flags, queries, own, left, right, glob, rand)


def split_kernel(k_ref, v_ref, o_ref):
    piece = o_ref.shape[4]
    for j in range(o_ref.shape[0]):
        o_ref[j, 0, 0] = k_ref[:, pl.ds(j * piece, piece)]
        o_ref[j, 0, 1] = v_ref[:, pl.ds(j * piece, piece)]


def split_pieces(key_rows, values, peers):
    rows, width = key_rows.shape
    piece = width // peers
    if piece % HEAD_DIM:
        keyvals = jnp.stack((key_rows, values))
        return keyvals.reshape(2, rows, peers, piece).transpose(2, 0, 1, 3)[:, None]
    per = max(1, min(peers, SPLIT_WIDTH // piece))
    while peers % per:
        per -= 1
    return pl.pallas_call(
        split_kernel,
        out_shape=jax.ShapeDtypeStruct((peers, 1, 2, rows, piece), key_rows.dtype),
        grid=(peers // per,),
        in_specs=[
            pl.BlockSpec((rows, per * piece), lambda j: (0, j)),
            pl.BlockSpec((rows, per * piece), lambda j: (0, j)),
        ],
        out_specs=pl.BlockSpec((per, 1, 2, rows, piece), lambda j: (j, 0, 0, 0, 0)),
    )(key_rows, values)


def feature_major(far):
    peers, count, two, rows, piece = far.shape
    return far.transpose(1, 2, 3, 0, 4).reshape(1, count, two, rows, peers * piece)


def per_device(queries, key_rows, values, random_ids, global_ids):
    tok_rows, feat_width = queries.shape
    peers = lax.axis_size("seq")
    my_rank = lax.axis_index("seq")
    local_blocks = tok_rows // BLK
    assert local_blocks == 1
    all_blocks = local_blocks * peers
    piece = feat_width // peers
    pieces = split_pieces(key_rows, values, peers)
    spread = lax.all_to_all(pieces, "seq", split_axis=0, concat_axis=0, tiled=True)
    spread = spread.reshape(all_blocks, 2, BLK, piece)
    outgoing = jnp.take(spread, random_ids.reshape(-1), axis=0, mode="clip")
    outgoing = outgoing.reshape(all_blocks, RAND, 2, BLK, piece)
    left = shifted(pieces, "seq", 1)
    right = shifted(pieces, "seq", -1)
    outgoing, left, right = lax.optimization_barrier((outgoing, left, right))
    rand = lax.all_to_all(outgoing, "seq", split_axis=0, concat_axis=0, tiled=True)
    glob_piece = jnp.take(spread, global_ids, axis=0, mode="clip")
    glob = lax.all_gather(glob_piece[None], "seq", axis=0, tiled=True)
    flags = jnp.stack((my_rank > 0, my_rank < peers - 1)).astype(jnp.int32)
    if piece % HEAD_DIM == 0:
        gw = GROUP * HEAD_DIM if (GROUP * HEAD_DIM) % piece == 0 else piece
    else:
        glob = feature_major(glob)
        rand = feature_major(rand)
        gw = GROUP * HEAD_DIM
    own = pieces
    if piece % HEAD_DIM:
        own = feature_major(own)
        left = feature_major(left)
        right = feature_major(right)
    return attend(flags, queries, own, left, right, glob, rand, gw)


def solution(mesh):
    return jax.shard_map(
        per_device,
        mesh=mesh,
        in_specs=(
            P(("grp", "seq"), None),
            P(("grp", "seq"), None),
            P(("grp", "seq"), None),
            P("grp", None),
            P("grp"),
        ),
        out_specs=P(("grp", "seq"), None),
        check_vma=False,
    )
```

```python
import functools
import math

import jax
import jax.numpy as jnp
from jax import lax
from jax.experimental import pallas as pl
from jax.experimental.pallas import tpu as pltpu
from jax.sharding import PartitionSpec as P

HEADS = 32
HEAD_DIM = 128
BLK = 128
RAND = 3
GLOBAL = 2
GROUP = 8
SPLIT_WIDTH = 1024

neg_big = -1e30


def shifted(block, axis, step):
    count = lax.axis_size(axis)
    if step > 0:
        pairs = [(i, i + 1) for i in range(count - 1)]
    else:
        pairs = [(i + 1, i) for i in range(count - 1)]
    return lax.ppermute(block, axis, pairs)


def early_kernel(flags_ref, q_ref, own_ref, left_ref, right_ref, glob_ref, w_ref, m_ref, d_ref, *, factor):
    left_ok = flags_ref[0] > 0
    right_ok = flags_ref[1] > 0
    rows = q_ref.shape[0]
    keys = (3 + glob_ref.shape[1]) * BLK
    col = lax.broadcasted_iota(jnp.int32, (rows, keys), 1)
    bad = ((col < BLK) & jnp.logical_not(left_ok)) | (
        (col >= 2 * BLK) & (col < 3 * BLK) & jnp.logical_not(right_ok)
    )
    piece_w = glob_ref.shape[4]
    for g in range(q_ref.shape[1] // HEAD_DIM):
        sl = pl.ds(g * HEAD_DIM, HEAD_DIM)
        src = (g * HEAD_DIM) // piece_w
        fsl = pl.ds((g * HEAD_DIM) % piece_w, HEAD_DIM)
        k_all = jnp.concatenate(
            (
                left_ref[src, 0, 0, :, fsl],
                own_ref[src, 0, 0, :, fsl],
                right_ref[src, 0, 0, :, fsl],
                *[glob_ref[src, j, 0, :, fsl] for j in range(glob_ref.shape[1])],
            ),
            axis=0,
        )
        scores = (
            lax.dot_general(
                q_ref[:, sl], k_all, (((1,), (1,)), ((), ())), preferred_element_type=jnp.float32
            )
            * factor
        )
        scores = jnp.where(bad, neg_big, scores)
        highest = jnp.max(scores, axis=-1, keepdims=True)
        weights = jnp.exp(scores - highest)
        w_ref[g] = weights
        m_ref[g] = highest
        d_ref[g] = jnp.sum(weights, axis=-1, keepdims=True)


def late_kernel(
    q_ref, own_ref, left_ref, right_ref, glob_ref, rand_ref, w_ref, m_ref, d_ref, o_ref, *, factor
):
    piece_w = rand_ref.shape[4]
    for g in range(q_ref.shape[1] // HEAD_DIM):
        sl = pl.ds(g * HEAD_DIM, HEAD_DIM)
        src = (g * HEAD_DIM) // piece_w
        fsl = pl.ds((g * HEAD_DIM) % piece_w, HEAD_DIM)
        k_far = jnp.concatenate(
            [rand_ref[src, j, 0, :, fsl] for j in range(rand_ref.shape[1])], axis=0
        )
        scores = (
            lax.dot_general(
                q_ref[:, sl], k_far, (((1,), (1,)), ((), ())), preferred_element_type=jnp.float32
            )
            * factor
        )
        early_max = m_ref[g]
        highest = jnp.maximum(early_max, jnp.max(scores, axis=-1, keepdims=True))
        scale = jnp.exp(early_max - highest)
        late_w = jnp.exp(scores - highest)
        denominator = d_ref[g] * scale + jnp.sum(late_w, axis=-1, keepdims=True)
        rounded = jnp.concatenate(
            ((w_ref[g] * scale).astype(jnp.bfloat16), late_w.astype(jnp.bfloat16)), axis=1
        )
        v_all = jnp.concatenate(
            (
                left_ref[src, 0, 1, :, fsl],
                own_ref[src, 0, 1, :, fsl],
                right_ref[src, 0, 1, :, fsl],
                *[glob_ref[src, j, 1, :, fsl] for j in range(glob_ref.shape[1])],
                *[rand_ref[src, j, 1, :, fsl] for j in range(rand_ref.shape[1])],
            ),
            axis=0,
        )
        mixed = jnp.dot(rounded, v_all, preferred_element_type=jnp.float32)
        o_ref[:, sl] = (mixed / denominator).astype(o_ref.dtype)


def far_spec(far, gw):
    width = far.shape[4]
    if width >= gw:
        per = width // gw
        return pl.BlockSpec(
            (1, far.shape[1], 2, BLK, gw), lambda h, *f: (h // per, 0, 0, 0, h % per)
        )
    return pl.BlockSpec(
        (gw // width, far.shape[1], 2, BLK, width), lambda h, *f: (h, 0, 0, 0, 0)
    )


def attend(flags, queries, own, left, right, glob, rand, gw):
    rows, width = queries.shape
    steps = width // gw
    heads = width // HEAD_DIM
    per_step = gw // HEAD_DIM
    early_keys = (3 + glob.shape[1]) * BLK
    factor = 1.0 / math.sqrt(HEAD_DIM)
    q_spec = pl.BlockSpec((rows, gw), lambda h, *f: (0, h))
    w_spec = pl.BlockSpec((per_step, rows, early_keys), lambda h, *f: (h, 0, 0))
    s_spec = pl.BlockSpec((per_step, rows, 1), lambda h, *f: (h, 0, 0))
    w, m, d = pl.pallas_call(
        functools.partial(early_kernel, factor=factor),
        out_shape=(
            jax.ShapeDtypeStruct((heads, rows, early_keys), jnp.float32),
            jax.ShapeDtypeStruct((heads, rows, 1), jnp.float32),
            jax.ShapeDtypeStruct((heads, rows, 1), jnp.float32),
        ),
        grid_spec=pltpu.PrefetchScalarGridSpec(
            num_scalar_prefetch=1,
            grid=(steps,),
            in_specs=[q_spec, far_spec(own, gw), far_spec(left, gw), far_spec(right, gw), far_spec(glob, gw)],
            out_specs=[w_spec, s_spec, s_spec],
        ),
    )(flags, queries, own, left, right, glob)
    return pl.pallas_call(
        functools.partial(late_kernel, factor=factor),
        out_shape=jax.ShapeDtypeStruct((rows, width), queries.dtype),
        grid=(steps,),
        in_specs=[
            q_spec,
            far_spec(own, gw),
            far_spec(left, gw),
            far_spec(right, gw),
            far_spec(glob, gw),
            far_spec(rand, gw),
            w_spec,
            s_spec,
            s_spec,
        ],
        out_specs=q_spec,
    )(queries, own, left, right, glob, rand, w, m, d)


def split_kernel(k_ref, v_ref, o_ref):
    piece = o_ref.shape[4]
    for j in range(o_ref.shape[0]):
        o_ref[j, 0, 0] = k_ref[:, pl.ds(j * piece, piece)]
        o_ref[j, 0, 1] = v_ref[:, pl.ds(j * piece, piece)]


def split_pieces(key_rows, values, peers):
    rows, width = key_rows.shape
    piece = width // peers
    if piece % HEAD_DIM:
        keyvals = jnp.stack((key_rows, values))
        return keyvals.reshape(2, rows, peers, piece).transpose(2, 0, 1, 3)[:, None]
    per = max(1, min(peers, SPLIT_WIDTH // piece))
    while peers % per:
        per -= 1
    return pl.pallas_call(
        split_kernel,
        out_shape=jax.ShapeDtypeStruct((peers, 1, 2, rows, piece), key_rows.dtype),
        grid=(peers // per,),
        in_specs=[
            pl.BlockSpec((rows, per * piece), lambda j: (0, j)),
            pl.BlockSpec((rows, per * piece), lambda j: (0, j)),
        ],
        out_specs=pl.BlockSpec((per, 1, 2, rows, piece), lambda j: (j, 0, 0, 0, 0)),
    )(key_rows, values)


def feature_major(far):
    peers, count, two, rows, piece = far.shape
    return far.transpose(1, 2, 3, 0, 4).reshape(1, count, two, rows, peers * piece)


def per_device(queries, key_rows, values, random_ids, global_ids):
    tok_rows, feat_width = queries.shape
    peers = lax.axis_size("seq")
    my_rank = lax.axis_index("seq")
    local_blocks = tok_rows // BLK
    assert local_blocks == 1
    all_blocks = local_blocks * peers
    piece = feat_width // peers
    pieces = split_pieces(key_rows, values, peers)
    spread = lax.all_to_all(pieces, "seq", split_axis=0, concat_axis=0, tiled=True)
    spread = spread.reshape(all_blocks, 2, BLK, piece)
    outgoing = jnp.take(spread, random_ids.reshape(-1), axis=0, mode="clip")
    outgoing = outgoing.reshape(all_blocks, RAND, 2, BLK, piece)
    left = shifted(pieces, "seq", 1)
    right = shifted(pieces, "seq", -1)
    outgoing, left, right = lax.optimization_barrier((outgoing, left, right))
    rand = lax.all_to_all(outgoing, "seq", split_axis=0, concat_axis=0, tiled=True)
    glob_piece = jnp.take(spread, global_ids, axis=0, mode="clip")
    glob = lax.all_gather(glob_piece[None], "seq", axis=0, tiled=True)
    flags = jnp.stack((my_rank > 0, my_rank < peers - 1)).astype(jnp.int32)
    if piece % HEAD_DIM == 0:
        gw = GROUP * HEAD_DIM if (GROUP * HEAD_DIM) % piece == 0 else piece
    else:
        glob = feature_major(glob)
        rand = feature_major(rand)
        gw = GROUP * HEAD_DIM
    own = pieces
    if piece % HEAD_DIM:
        own = feature_major(own)
        left = feature_major(left)
        right = feature_major(right)
    return attend(flags, queries, own, left, right, glob, rand, gw)


def solution(mesh):
    return jax.shard_map(
        per_device,
        mesh=mesh,
        in_specs=(
            P(("grp", "seq"), None),
            P(("grp", "seq"), None),
            P(("grp", "seq"), None),
            P("grp", None),
            P("grp"),
        ),
        out_specs=P(("grp", "seq"), None),
        check_vma=False,
    )
```

```python
import functools
import math

import jax
import jax.numpy as jnp
from jax import lax
from jax.experimental import pallas as pl
from jax.experimental.pallas import tpu as pltpu
from jax.sharding import PartitionSpec as P

HEADS = 32
HEAD_DIM = 128
BLK = 128
RAND = 3
GLOBAL = 2
GROUP = 8
SPLIT_WIDTH = 1024

neg_big = -1e30


def shifted(block, axis, step):
    count = lax.axis_size(axis)
    if step > 0:
        pairs = [(i, i + 1) for i in range(count - 1)]
    else:
        pairs = [(i + 1, i) for i in range(count - 1)]
    return lax.ppermute(block, axis, pairs)


def attend_kernel(
    flags_ref, q_ref, own_ref, left_ref, right_ref, glob_ref, rand_ref, o_ref, *, factor
):
    left_ok = flags_ref[0] > 0
    right_ok = flags_ref[1] > 0
    rows = q_ref.shape[0]
    far_count = glob_ref.shape[1] + rand_ref.shape[1]
    keys = (3 + far_count) * BLK
    col = lax.broadcasted_iota(jnp.int32, (rows, keys), 1)
    bad = ((col < BLK) & jnp.logical_not(left_ok)) | (
        (col >= 2 * BLK) & (col < 3 * BLK) & jnp.logical_not(right_ok)
    )
    piece_w = glob_ref.shape[4]
    for g in range(q_ref.shape[1] // HEAD_DIM):
        sl = pl.ds(g * HEAD_DIM, HEAD_DIM)
        src = (g * HEAD_DIM) // piece_w
        fsl = pl.ds((g * HEAD_DIM) % piece_w, HEAD_DIM)
        qh = q_ref[:, sl]
        k_all = jnp.concatenate(
            (
                left_ref[src, 0, 0, :, fsl],
                own_ref[src, 0, 0, :, fsl],
                right_ref[src, 0, 0, :, fsl],
                *[glob_ref[src, j, 0, :, fsl] for j in range(glob_ref.shape[1])],
                *[rand_ref[src, j, 0, :, fsl] for j in range(rand_ref.shape[1])],
            ),
            axis=0,
        )
        scores = (
            lax.dot_general(
                qh, k_all, (((1,), (1,)), ((), ())), preferred_element_type=jnp.float32
            )
            * factor
        )
        scores = jnp.where(bad, neg_big, scores)
        highest = jnp.max(scores, axis=-1, keepdims=True)
        weights = jnp.exp(scores - highest)
        denominator = jnp.sum(weights, axis=-1, keepdims=True)
        v_all = jnp.concatenate(
            (
                left_ref[src, 0, 1, :, fsl],
                own_ref[src, 0, 1, :, fsl],
                right_ref[src, 0, 1, :, fsl],
                *[glob_ref[src, j, 1, :, fsl] for j in range(glob_ref.shape[1])],
                *[rand_ref[src, j, 1, :, fsl] for j in range(rand_ref.shape[1])],
            ),
            axis=0,
        )
        mixed = jnp.dot(weights.astype(jnp.bfloat16), v_all, preferred_element_type=jnp.float32)
        o_ref[:, sl] = (mixed / denominator).astype(o_ref.dtype)


def far_spec(far, gw):
    width = far.shape[4]
    if width >= gw:
        per = width // gw
        return pl.BlockSpec(
            (1, far.shape[1], 2, BLK, gw), lambda h, f: (h // per, 0, 0, 0, h % per)
        )
    return pl.BlockSpec(
        (gw // width, far.shape[1], 2, BLK, width), lambda h, f: (h, 0, 0, 0, 0)
    )


def attend(flags, queries, own, left, right, glob, rand, gw):
    rows, width = queries.shape
    steps = width // gw
    kernel = functools.partial(attend_kernel, factor=1.0 / math.sqrt(HEAD_DIM))
    return pl.pallas_call(
        kernel,
        out_shape=jax.ShapeDtypeStruct((rows, width), queries.dtype),
        grid_spec=pltpu.PrefetchScalarGridSpec(
            num_scalar_prefetch=1,
            grid=(steps,),
            in_specs=[
                pl.BlockSpec((rows, gw), lambda h, f: (0, h)),
                far_spec(own, gw),
                far_spec(left, gw),
                far_spec(right, gw),
                far_spec(glob, gw),
                far_spec(rand, gw),
            ],
            out_specs=pl.BlockSpec((rows, gw), lambda h, f: (0, h)),
        ),
    )(flags, queries, own, left, right, glob, rand)


def split_kernel(k_ref, v_ref, o_ref):
    piece = o_ref.shape[4]
    for j in range(o_ref.shape[0]):
        o_ref[j, 0, 0] = k_ref[:, pl.ds(j * piece, piece)]
        o_ref[j, 0, 1] = v_ref[:, pl.ds(j * piece, piece)]


def split_pieces(key_rows, values, peers):
    rows, width = key_rows.shape
    piece = width // peers
    if piece % HEAD_DIM:
        keyvals = jnp.stack((key_rows, values))
        return keyvals.reshape(2, rows, peers, piece).transpose(2, 0, 1, 3)[:, None]
    per = max(1, min(peers, SPLIT_WIDTH // piece))
    while peers % per:
        per -= 1
    return pl.pallas_call(
        split_kernel,
        out_shape=jax.ShapeDtypeStruct((peers, 1, 2, rows, piece), key_rows.dtype),
        grid=(peers // per,),
        in_specs=[
            pl.BlockSpec((rows, per * piece), lambda j: (0, j)),
            pl.BlockSpec((rows, per * piece), lambda j: (0, j)),
        ],
        out_specs=pl.BlockSpec((per, 1, 2, rows, piece), lambda j: (j, 0, 0, 0, 0)),
    )(key_rows, values)


def feature_major(far):
    peers, count, two, rows, piece = far.shape
    return far.transpose(1, 2, 3, 0, 4).reshape(1, count, two, rows, peers * piece)


def per_device(queries, key_rows, values, random_ids, global_ids):
    tok_rows, feat_width = queries.shape
    peers = lax.axis_size("seq")
    my_rank = lax.axis_index("seq")
    local_blocks = tok_rows // BLK
    assert local_blocks == 1
    all_blocks = local_blocks * peers
    piece = feat_width // peers
    pieces = split_pieces(key_rows, values, peers)
    spread = lax.all_to_all(pieces, "seq", split_axis=0, concat_axis=0, tiled=True)
    spread = spread.reshape(all_blocks, 2, BLK, piece)
    outgoing = jnp.take(spread, random_ids.reshape(-1), axis=0, mode="clip")
    outgoing = outgoing.reshape(all_blocks, RAND, 2, BLK, piece)
    rand = lax.all_to_all(outgoing, "seq", split_axis=0, concat_axis=0, tiled=True)
    left = shifted(pieces, "seq", 1)
    right = shifted(pieces, "seq", -1)
    glob_piece = jnp.take(spread, global_ids, axis=0, mode="clip")
    glob_piece, left, right = lax.optimization_barrier((glob_piece, left, right))
    glob = lax.all_gather(glob_piece[None], "seq", axis=0, tiled=True)
    flags = jnp.stack((my_rank > 0, my_rank < peers - 1)).astype(jnp.int32)
    if piece % HEAD_DIM == 0:
        gw = GROUP * HEAD_DIM if (GROUP * HEAD_DIM) % piece == 0 else piece
    else:
        glob = feature_major(glob)
        rand = feature_major(rand)
        gw = GROUP * HEAD_DIM
    own = pieces
    if piece % HEAD_DIM:
        own = feature_major(own)
        left = feature_major(left)
        right = feature_major(right)
    return attend(flags, queries, own, left, right, glob, rand, gw)


def solution(mesh):
    return jax.shard_map(
        per_device,
        mesh=mesh,
        in_specs=(
            P(("grp", "seq"), None),
            P(("grp", "seq"), None),
            P(("grp", "seq"), None),
            P("grp", None),
            P("grp"),
        ),
        out_specs=P(("grp", "seq"), None),
        check_vma=False,
    )
```

```python
import functools
import math

import jax
import jax.numpy as jnp
from jax import lax
from jax.experimental import pallas as pl
from jax.experimental.pallas import tpu as pltpu
from jax.sharding import PartitionSpec as P

HEADS = 32
HEAD_DIM = 128
BLK = 128
RAND = 3
GLOBAL = 2
GROUP = 8
SPLIT_WIDTH = 1024

neg_big = -1e30


def shifted(block, axis, step):
    count = lax.axis_size(axis)
    if step > 0:
        pairs = [(i, i + 1) for i in range(count - 1)]
    else:
        pairs = [(i + 1, i) for i in range(count - 1)]
    return lax.ppermute(block, axis, pairs)


def attend_kernel(
    flags_ref, q_ref, own_ref, left_ref, right_ref, glob_ref, rand_ref, o_ref, *, factor
):
    left_ok = flags_ref[0] > 0
    right_ok = flags_ref[1] > 0
    rows = q_ref.shape[0]
    far_count = glob_ref.shape[1] + rand_ref.shape[1]
    keys = (3 + far_count) * BLK
    col = lax.broadcasted_iota(jnp.int32, (1, keys), 1)
    bad = ((col < BLK) & jnp.logical_not(left_ok)) | (
        (col >= 2 * BLK) & (col < 3 * BLK) & jnp.logical_not(right_ok)
    )
    bias = jnp.where(bad, neg_big, 0.0).astype(jnp.float32)
    piece_w = glob_ref.shape[4]
    for g in range(q_ref.shape[1] // HEAD_DIM):
        sl = pl.ds(g * HEAD_DIM, HEAD_DIM)
        src = (g * HEAD_DIM) // piece_w
        fsl = pl.ds((g * HEAD_DIM) % piece_w, HEAD_DIM)
        qh = q_ref[:, sl]
        k_all = jnp.concatenate(
            (
                left_ref[src, 0, 0, :, fsl],
                own_ref[src, 0, 0, :, fsl],
                right_ref[src, 0, 0, :, fsl],
                *[glob_ref[src, j, 0, :, fsl] for j in range(glob_ref.shape[1])],
                *[rand_ref[src, j, 0, :, fsl] for j in range(rand_ref.shape[1])],
            ),
            axis=0,
        )
        scores = (
            lax.dot_general(
                qh, k_all, (((1,), (1,)), ((), ())), preferred_element_type=jnp.float32
            )
            * factor
            + bias
        )
        highest = jnp.max(scores, axis=-1, keepdims=True)
        weights = jnp.exp(scores - highest)
        denominator = jnp.sum(weights, axis=-1, keepdims=True)
        v_all = jnp.concatenate(
            (
                left_ref[src, 0, 1, :, fsl],
                own_ref[src, 0, 1, :, fsl],
                right_ref[src, 0, 1, :, fsl],
                *[glob_ref[src, j, 1, :, fsl] for j in range(glob_ref.shape[1])],
                *[rand_ref[src, j, 1, :, fsl] for j in range(rand_ref.shape[1])],
            ),
            axis=0,
        )
        mixed = jnp.dot(weights.astype(jnp.bfloat16), v_all, preferred_element_type=jnp.float32)
        o_ref[:, sl] = (mixed / denominator).astype(o_ref.dtype)


def far_spec(far, gw):
    width = far.shape[4]
    if width >= gw:
        per = width // gw
        return pl.BlockSpec(
            (1, far.shape[1], 2, BLK, gw), lambda h, f: (h // per, 0, 0, 0, h % per)
        )
    return pl.BlockSpec(
        (gw // width, far.shape[1], 2, BLK, width), lambda h, f: (h, 0, 0, 0, 0)
    )


def attend(flags, queries, own, left, right, glob, rand, gw):
    rows, width = queries.shape
    steps = width // gw
    kernel = functools.partial(attend_kernel, factor=1.0 / math.sqrt(HEAD_DIM))
    return pl.pallas_call(
        kernel,
        out_shape=jax.ShapeDtypeStruct((rows, width), queries.dtype),
        grid_spec=pltpu.PrefetchScalarGridSpec(
            num_scalar_prefetch=1,
            grid=(steps,),
            in_specs=[
                pl.BlockSpec((rows, gw), lambda h, f: (0, h)),
                far_spec(own, gw),
                far_spec(left, gw),
                far_spec(right, gw),
                far_spec(glob, gw),
                far_spec(rand, gw),
            ],
            out_specs=pl.BlockSpec((rows, gw), lambda h, f: (0, h)),
        ),
    )(flags, queries, own, left, right, glob, rand)


def split_kernel(k_ref, v_ref, o_ref):
    piece = o_ref.shape[4]
    for j in range(o_ref.shape[0]):
        o_ref[j, 0, 0] = k_ref[:, pl.ds(j * piece, piece)]
        o_ref[j, 0, 1] = v_ref[:, pl.ds(j * piece, piece)]


def split_pieces(key_rows, values, peers):
    rows, width = key_rows.shape
    piece = width // peers
    if piece % HEAD_DIM:
        keyvals = jnp.stack((key_rows, values))
        return keyvals.reshape(2, rows, peers, piece).transpose(2, 0, 1, 3)[:, None]
    per = max(1, min(peers, SPLIT_WIDTH // piece))
    while peers % per:
        per -= 1
    return pl.pallas_call(
        split_kernel,
        out_shape=jax.ShapeDtypeStruct((peers, 1, 2, rows, piece), key_rows.dtype),
        grid=(peers // per,),
        in_specs=[
            pl.BlockSpec((rows, per * piece), lambda j: (0, j)),
            pl.BlockSpec((rows, per * piece), lambda j: (0, j)),
        ],
        out_specs=pl.BlockSpec((per, 1, 2, rows, piece), lambda j: (j, 0, 0, 0, 0)),
    )(key_rows, values)


def feature_major(far):
    peers, count, two, rows, piece = far.shape
    return far.transpose(1, 2, 3, 0, 4).reshape(1, count, two, rows, peers * piece)


def per_device(queries, key_rows, values, random_ids, global_ids):
    tok_rows, feat_width = queries.shape
    peers = lax.axis_size("seq")
    my_rank = lax.axis_index("seq")
    local_blocks = tok_rows // BLK
    assert local_blocks == 1
    all_blocks = local_blocks * peers
    piece = feat_width // peers
    pieces = split_pieces(key_rows, values, peers)
    spread = lax.all_to_all(pieces, "seq", split_axis=0, concat_axis=0, tiled=True)
    spread = spread.reshape(all_blocks, 2, BLK, piece)
    outgoing = jnp.take(spread, random_ids.reshape(-1), axis=0, mode="clip")
    outgoing = outgoing.reshape(all_blocks, RAND, 2, BLK, piece)
    left = shifted(pieces, "seq", 1)
    right = shifted(pieces, "seq", -1)
    outgoing, left, right = lax.optimization_barrier((outgoing, left, right))
    rand = lax.all_to_all(outgoing, "seq", split_axis=0, concat_axis=0, tiled=True)
    glob_piece = jnp.take(spread, global_ids, axis=0, mode="clip")
    glob = lax.all_gather(glob_piece[None], "seq", axis=0, tiled=True)
    flags = jnp.stack((my_rank > 0, my_rank < peers - 1)).astype(jnp.int32)
    if piece % HEAD_DIM == 0:
        gw = GROUP * HEAD_DIM if (GROUP * HEAD_DIM) % piece == 0 else piece
    else:
        glob = feature_major(glob)
        rand = feature_major(rand)
        gw = GROUP * HEAD_DIM
    own = pieces
    if piece % HEAD_DIM:
        own = feature_major(own)
        left = feature_major(left)
        right = feature_major(right)
    return attend(flags, queries, own, left, right, glob, rand, gw)


def solution(mesh):
    return jax.shard_map(
        per_device,
        mesh=mesh,
        in_specs=(
            P(("grp", "seq"), None),
            P(("grp", "seq"), None),
            P(("grp", "seq"), None),
            P("grp", None),
            P("grp"),
        ),
        out_specs=P(("grp", "seq"), None),
        check_vma=False,
    )
```

```python
import functools
import math

import jax
import jax.numpy as jnp
from jax import lax
from jax.experimental import pallas as pl
from jax.experimental.pallas import tpu as pltpu
from jax.sharding import PartitionSpec as P

HEADS = 32
HEAD_DIM = 128
BLK = 128
RAND = 3
GLOBAL = 2
GROUP = 8
SPLIT_WIDTH = 2048

neg_big = -1e30


def shifted(block, axis, step):
    count = lax.axis_size(axis)
    if step > 0:
        pairs = [(i, i + 1) for i in range(count - 1)]
    else:
        pairs = [(i + 1, i) for i in range(count - 1)]
    return lax.ppermute(block, axis, pairs)


def attend_kernel(
    flags_ref, q_ref, own_ref, left_ref, right_ref, glob_ref, rand_ref, o_ref, *, factor
):
    left_ok = flags_ref[0] > 0
    right_ok = flags_ref[1] > 0
    rows = q_ref.shape[0]
    far_count = glob_ref.shape[1] + rand_ref.shape[1]
    keys = (3 + far_count) * BLK
    col = lax.broadcasted_iota(jnp.int32, (rows, keys), 1)
    bad = ((col < BLK) & jnp.logical_not(left_ok)) | (
        (col >= 2 * BLK) & (col < 3 * BLK) & jnp.logical_not(right_ok)
    )
    piece_w = glob_ref.shape[4]
    for g in range(q_ref.shape[1] // HEAD_DIM):
        sl = pl.ds(g * HEAD_DIM, HEAD_DIM)
        src = (g * HEAD_DIM) // piece_w
        fsl = pl.ds((g * HEAD_DIM) % piece_w, HEAD_DIM)
        qh = q_ref[:, sl]
        k_all = jnp.concatenate(
            (
                left_ref[src, 0, 0, :, fsl],
                own_ref[src, 0, 0, :, fsl],
                right_ref[src, 0, 0, :, fsl],
                *[glob_ref[src, j, 0, :, fsl] for j in range(glob_ref.shape[1])],
                *[rand_ref[src, j, 0, :, fsl] for j in range(rand_ref.shape[1])],
            ),
            axis=0,
        )
        scores = (
            lax.dot_general(
                qh, k_all, (((1,), (1,)), ((), ())), preferred_element_type=jnp.float32
            )
            * factor
        )
        scores = jnp.where(bad, neg_big, scores)
        highest = jnp.max(scores, axis=-1, keepdims=True)
        weights = jnp.exp(scores - highest)
        denominator = jnp.sum(weights, axis=-1, keepdims=True)
        v_all = jnp.concatenate(
            (
                left_ref[src, 0, 1, :, fsl],
                own_ref[src, 0, 1, :, fsl],
                right_ref[src, 0, 1, :, fsl],
                *[glob_ref[src, j, 1, :, fsl] for j in range(glob_ref.shape[1])],
                *[rand_ref[src, j, 1, :, fsl] for j in range(rand_ref.shape[1])],
            ),
            axis=0,
        )
        mixed = jnp.dot(weights.astype(jnp.bfloat16), v_all, preferred_element_type=jnp.float32)
        o_ref[:, sl] = (mixed / denominator).astype(o_ref.dtype)


def far_spec(far, gw):
    width = far.shape[4]
    if width >= gw:
        per = width // gw
        return pl.BlockSpec(
            (1, far.shape[1], 2, BLK, gw), lambda h, f: (h // per, 0, 0, 0, h % per)
        )
    return pl.BlockSpec(
        (gw // width, far.shape[1], 2, BLK, width), lambda h, f: (h, 0, 0, 0, 0)
    )


def attend(flags, queries, own, left, right, glob, rand, gw):
    rows, width = queries.shape
    steps = width // gw
    kernel = functools.partial(attend_kernel, factor=1.0 / math.sqrt(HEAD_DIM))
    return pl.pallas_call(
        kernel,
        out_shape=jax.ShapeDtypeStruct((rows, width), queries.dtype),
        grid_spec=pltpu.PrefetchScalarGridSpec(
            num_scalar_prefetch=1,
            grid=(steps,),
            in_specs=[
                pl.BlockSpec((rows, gw), lambda h, f: (0, h)),
                far_spec(own, gw),
                far_spec(left, gw),
                far_spec(right, gw),
                far_spec(glob, gw),
                far_spec(rand, gw),
            ],
            out_specs=pl.BlockSpec((rows, gw), lambda h, f: (0, h)),
        ),
    )(flags, queries, own, left, right, glob, rand)


def split_kernel(k_ref, v_ref, o_ref):
    piece = o_ref.shape[4]
    for j in range(o_ref.shape[0]):
        o_ref[j, 0, 0] = k_ref[:, pl.ds(j * piece, piece)]
        o_ref[j, 0, 1] = v_ref[:, pl.ds(j * piece, piece)]


def split_pieces(key_rows, values, peers):
    rows, width = key_rows.shape
    piece = width // peers
    if piece % HEAD_DIM:
        keyvals = jnp.stack((key_rows, values))
        return keyvals.reshape(2, rows, peers, piece).transpose(2, 0, 1, 3)[:, None]
    per = max(1, min(peers, SPLIT_WIDTH // piece))
    while peers % per:
        per -= 1
    return pl.pallas_call(
        split_kernel,
        out_shape=jax.ShapeDtypeStruct((peers, 1, 2, rows, piece), key_rows.dtype),
        grid=(peers // per,),
        in_specs=[
            pl.BlockSpec((rows, per * piece), lambda j: (0, j)),
            pl.BlockSpec((rows, per * piece), lambda j: (0, j)),
        ],
        out_specs=pl.BlockSpec((per, 1, 2, rows, piece), lambda j: (j, 0, 0, 0, 0)),
    )(key_rows, values)


def feature_major(far):
    peers, count, two, rows, piece = far.shape
    return far.transpose(1, 2, 3, 0, 4).reshape(1, count, two, rows, peers * piece)


def per_device(queries, key_rows, values, random_ids, global_ids):
    tok_rows, feat_width = queries.shape
    peers = lax.axis_size("seq")
    my_rank = lax.axis_index("seq")
    local_blocks = tok_rows // BLK
    assert local_blocks == 1
    all_blocks = local_blocks * peers
    piece = feat_width // peers
    pieces = split_pieces(key_rows, values, peers)
    spread = lax.all_to_all(pieces, "seq", split_axis=0, concat_axis=0, tiled=True)
    spread = spread.reshape(all_blocks, 2, BLK, piece)
    outgoing = jnp.take(spread, random_ids.reshape(-1), axis=0, mode="clip")
    outgoing = outgoing.reshape(all_blocks, RAND, 2, BLK, piece)
    left = shifted(pieces, "seq", 1)
    right = shifted(pieces, "seq", -1)
    outgoing, left, right = lax.optimization_barrier((outgoing, left, right))
    rand = lax.all_to_all(outgoing, "seq", split_axis=0, concat_axis=0, tiled=True)
    glob_piece = jnp.take(spread, global_ids, axis=0, mode="clip")
    glob = lax.all_gather(glob_piece[None], "seq", axis=0, tiled=True)
    flags = jnp.stack((my_rank > 0, my_rank < peers - 1)).astype(jnp.int32)
    if piece % HEAD_DIM == 0:
        gw = GROUP * HEAD_DIM if (GROUP * HEAD_DIM) % piece == 0 else piece
    else:
        glob = feature_major(glob)
        rand = feature_major(rand)
        gw = GROUP * HEAD_DIM
    own = pieces
    if piece % HEAD_DIM:
        own = feature_major(own)
        left = feature_major(left)
        right = feature_major(right)
    return attend(flags, queries, own, left, right, glob, rand, gw)


def solution(mesh):
    return jax.shard_map(
        per_device,
        mesh=mesh,
        in_specs=(
            P(("grp", "seq"), None),
            P(("grp", "seq"), None),
            P(("grp", "seq"), None),
            P("grp", None),
            P("grp"),
        ),
        out_specs=P(("grp", "seq"), None),
        check_vma=False,
    )
```

```python
import functools
import math

import jax
import jax.numpy as jnp
from jax import lax
from jax.experimental import pallas as pl
from jax.experimental.pallas import tpu as pltpu
from jax.sharding import PartitionSpec as P

HEADS = 32
HEAD_DIM = 128
BLK = 128
RAND = 3
GLOBAL = 2
GROUP = 16
SPLIT_WIDTH = 2048

neg_big = -1e30


def shifted(block, axis, step):
    count = lax.axis_size(axis)
    if step > 0:
        pairs = [(i, i + 1) for i in range(count - 1)]
    else:
        pairs = [(i + 1, i) for i in range(count - 1)]
    return lax.ppermute(block, axis, pairs)


def attend_kernel(
    flags_ref, q_ref, own_ref, left_ref, right_ref, glob_ref, rand_ref, o_ref, *, factor
):
    left_ok = flags_ref[0] > 0
    right_ok = flags_ref[1] > 0
    rows = q_ref.shape[0]
    far_count = glob_ref.shape[1] + rand_ref.shape[1]
    keys = (3 + far_count) * BLK
    col = lax.broadcasted_iota(jnp.int32, (rows, keys), 1)
    bad = ((col < BLK) & jnp.logical_not(left_ok)) | (
        (col >= 2 * BLK) & (col < 3 * BLK) & jnp.logical_not(right_ok)
    )
    piece_w = glob_ref.shape[4]
    for g in range(q_ref.shape[1] // HEAD_DIM):
        sl = pl.ds(g * HEAD_DIM, HEAD_DIM)
        src = (g * HEAD_DIM) // piece_w
        fsl = pl.ds((g * HEAD_DIM) % piece_w, HEAD_DIM)
        qh = q_ref[:, sl]
        k_all = jnp.concatenate(
            (
                left_ref[src, 0, 0, :, fsl],
                own_ref[src, 0, 0, :, fsl],
                right_ref[src, 0, 0, :, fsl],
                *[glob_ref[src, j, 0, :, fsl] for j in range(glob_ref.shape[1])],
                *[rand_ref[src, j, 0, :, fsl] for j in range(rand_ref.shape[1])],
            ),
            axis=0,
        )
        scores = (
            lax.dot_general(
                qh, k_all, (((1,), (1,)), ((), ())), preferred_element_type=jnp.float32
            )
            * factor
        )
        scores = jnp.where(bad, neg_big, scores)
        highest = jnp.max(scores, axis=-1, keepdims=True)
        weights = jnp.exp(scores - highest)
        denominator = jnp.sum(weights, axis=-1, keepdims=True)
        v_all = jnp.concatenate(
            (
                left_ref[src, 0, 1, :, fsl],
                own_ref[src, 0, 1, :, fsl],
                right_ref[src, 0, 1, :, fsl],
                *[glob_ref[src, j, 1, :, fsl] for j in range(glob_ref.shape[1])],
                *[rand_ref[src, j, 1, :, fsl] for j in range(rand_ref.shape[1])],
            ),
            axis=0,
        )
        mixed = jnp.dot(weights.astype(jnp.bfloat16), v_all, preferred_element_type=jnp.float32)
        o_ref[:, sl] = (mixed / denominator).astype(o_ref.dtype)


def far_spec(far, gw):
    width = far.shape[4]
    if width >= gw:
        per = width // gw
        return pl.BlockSpec(
            (1, far.shape[1], 2, BLK, gw), lambda h, f: (h // per, 0, 0, 0, h % per)
        )
    return pl.BlockSpec(
        (gw // width, far.shape[1], 2, BLK, width), lambda h, f: (h, 0, 0, 0, 0)
    )


def attend(flags, queries, own, left, right, glob, rand, gw):
    rows, width = queries.shape
    steps = width // gw
    kernel = functools.partial(attend_kernel, factor=1.0 / math.sqrt(HEAD_DIM))
    return pl.pallas_call(
        kernel,
        out_shape=jax.ShapeDtypeStruct((rows, width), queries.dtype),
        grid_spec=pltpu.PrefetchScalarGridSpec(
            num_scalar_prefetch=1,
            grid=(steps,),
            in_specs=[
                pl.BlockSpec((rows, gw), lambda h, f: (0, h)),
                far_spec(own, gw),
                far_spec(left, gw),
                far_spec(right, gw),
                far_spec(glob, gw),
                far_spec(rand, gw),
            ],
            out_specs=pl.BlockSpec((rows, gw), lambda h, f: (0, h)),
        ),
    )(flags, queries, own, left, right, glob, rand)


def split_kernel(k_ref, v_ref, o_ref):
    piece = o_ref.shape[4]
    for j in range(o_ref.shape[0]):
        o_ref[j, 0, 0] = k_ref[:, pl.ds(j * piece, piece)]
        o_ref[j, 0, 1] = v_ref[:, pl.ds(j * piece, piece)]


def split_pieces(key_rows, values, peers):
    rows, width = key_rows.shape
    piece = width // peers
    if piece % HEAD_DIM:
        keyvals = jnp.stack((key_rows, values))
        return keyvals.reshape(2, rows, peers, piece).transpose(2, 0, 1, 3)[:, None]
    per = max(1, min(peers, SPLIT_WIDTH // piece))
    while peers % per:
        per -= 1
    return pl.pallas_call(
        split_kernel,
        out_shape=jax.ShapeDtypeStruct((peers, 1, 2, rows, piece), key_rows.dtype),
        grid=(peers // per,),
        in_specs=[
            pl.BlockSpec((rows, per * piece), lambda j: (0, j)),
            pl.BlockSpec((rows, per * piece), lambda j: (0, j)),
        ],
        out_specs=pl.BlockSpec((per, 1, 2, rows, piece), lambda j: (j, 0, 0, 0, 0)),
    )(key_rows, values)


def feature_major(far):
    peers, count, two, rows, piece = far.shape
    return far.transpose(1, 2, 3, 0, 4).reshape(1, count, two, rows, peers * piece)


def per_device(queries, key_rows, values, random_ids, global_ids):
    tok_rows, feat_width = queries.shape
    peers = lax.axis_size("seq")
    my_rank = lax.axis_index("seq")
    local_blocks = tok_rows // BLK
    assert local_blocks == 1
    all_blocks = local_blocks * peers
    piece = feat_width // peers
    pieces = split_pieces(key_rows, values, peers)
    spread = lax.all_to_all(pieces, "seq", split_axis=0, concat_axis=0, tiled=True)
    spread = spread.reshape(all_blocks, 2, BLK, piece)
    outgoing = jnp.take(spread, random_ids.reshape(-1), axis=0, mode="clip")
    outgoing = outgoing.reshape(all_blocks, RAND, 2, BLK, piece)
    left = shifted(pieces, "seq", 1)
    right = shifted(pieces, "seq", -1)
    outgoing, left, right = lax.optimization_barrier((outgoing, left, right))
    rand = lax.all_to_all(outgoing, "seq", split_axis=0, concat_axis=0, tiled=True)
    glob_piece = jnp.take(spread, global_ids, axis=0, mode="clip")
    glob = lax.all_gather(glob_piece[None], "seq", axis=0, tiled=True)
    flags = jnp.stack((my_rank > 0, my_rank < peers - 1)).astype(jnp.int32)
    if piece % HEAD_DIM == 0:
        gw = GROUP * HEAD_DIM if (GROUP * HEAD_DIM) % piece == 0 else piece
    else:
        glob = feature_major(glob)
        rand = feature_major(rand)
        gw = GROUP * HEAD_DIM
    own = pieces
    if piece % HEAD_DIM:
        own = feature_major(own)
        left = feature_major(left)
        right = feature_major(right)
    return attend(flags, queries, own, left, right, glob, rand, gw)


def solution(mesh):
    return jax.shard_map(
        per_device,
        mesh=mesh,
        in_specs=(
            P(("grp", "seq"), None),
            P(("grp", "seq"), None),
            P(("grp", "seq"), None),
            P("grp", None),
            P("grp"),
        ),
        out_specs=P(("grp", "seq"), None),
        check_vma=False,
    )
```

```python
import functools
import math

import jax
import jax.numpy as jnp
from jax import lax
from jax.experimental import pallas as pl
from jax.experimental.pallas import tpu as pltpu
from jax.sharding import PartitionSpec as P

HEADS = 32
HEAD_DIM = 128
BLK = 128
RAND = 3
GLOBAL = 2
GROUP = 8
SPLIT_WIDTH = 2048

neg_big = -1e30


def shifted(block, axis, step):
    count = lax.axis_size(axis)
    if step > 0:
        pairs = [(i, i + 1) for i in range(count - 1)]
    else:
        pairs = [(i + 1, i) for i in range(count - 1)]
    return lax.ppermute(block, axis, pairs)


def early_kernel(
    flags_ref, q_ref, own_ref, left_ref, right_ref, glob_ref, o_ref, m_ref, d_ref, *, factor
):
    left_ok = flags_ref[0] > 0
    right_ok = flags_ref[1] > 0
    keys = (3 + glob_ref.shape[1]) * BLK
    col = lax.broadcasted_iota(jnp.int32, (1, keys), 1)
    bad = ((col < BLK) & jnp.logical_not(left_ok)) | (
        (col >= 2 * BLK) & (col < 3 * BLK) & jnp.logical_not(right_ok)
    )
    bias = jnp.where(bad, neg_big, 0.0).astype(jnp.float32)
    piece_w = glob_ref.shape[4]
    for g in range(q_ref.shape[1] // HEAD_DIM):
        sl = pl.ds(g * HEAD_DIM, HEAD_DIM)
        src = (g * HEAD_DIM) // piece_w
        fsl = pl.ds((g * HEAD_DIM) % piece_w, HEAD_DIM)
        near = (left_ref, own_ref, right_ref)
        k_all = jnp.concatenate(
            (
                *[ref[src, 0, 0, :, fsl] for ref in near],
                *[glob_ref[src, j, 0, :, fsl] for j in range(glob_ref.shape[1])],
            ),
            axis=0,
        )
        scores = (
            lax.dot_general(
                q_ref[:, sl], k_all, (((1,), (1,)), ((), ())), preferred_element_type=jnp.float32
            )
            * factor
            + bias
        )
        highest = jnp.max(scores, axis=-1, keepdims=True)
        weights = jnp.exp(scores - highest)
        v_all = jnp.concatenate(
            (
                *[ref[src, 0, 1, :, fsl] for ref in near],
                *[glob_ref[src, j, 1, :, fsl] for j in range(glob_ref.shape[1])],
            ),
            axis=0,
        )
        o_ref[g] = jnp.dot(weights.astype(jnp.bfloat16), v_all, preferred_element_type=jnp.float32)
        m_ref[g] = highest
        d_ref[g] = jnp.sum(weights, axis=-1, keepdims=True)


def late_kernel(q_ref, rand_ref, part_ref, m_ref, d_ref, o_ref, *, factor):
    piece_w = rand_ref.shape[4]
    for g in range(q_ref.shape[1] // HEAD_DIM):
        sl = pl.ds(g * HEAD_DIM, HEAD_DIM)
        src = (g * HEAD_DIM) // piece_w
        fsl = pl.ds((g * HEAD_DIM) % piece_w, HEAD_DIM)
        count = rand_ref.shape[1]
        k_far = jnp.concatenate([rand_ref[src, j, 0, :, fsl] for j in range(count)], axis=0)
        v_far = jnp.concatenate([rand_ref[src, j, 1, :, fsl] for j in range(count)], axis=0)
        scores = (
            lax.dot_general(
                q_ref[:, sl], k_far, (((1,), (1,)), ((), ())), preferred_element_type=jnp.float32
            )
            * factor
        )
        early_max = m_ref[g]
        highest = jnp.maximum(early_max, jnp.max(scores, axis=-1, keepdims=True))
        scale = jnp.exp(early_max - highest)
        weights = jnp.exp(scores - highest)
        denominator = d_ref[g] * scale + jnp.sum(weights, axis=-1, keepdims=True)
        mixed = part_ref[g] * scale + jnp.dot(
            weights.astype(jnp.bfloat16), v_far, preferred_element_type=jnp.float32
        )
        o_ref[:, sl] = (mixed / denominator).astype(o_ref.dtype)


def far_spec(far, gw):
    width = far.shape[4]
    if width >= gw:
        per = width // gw
        return pl.BlockSpec(
            (1, far.shape[1], 2, BLK, gw), lambda h, *f: (h // per, 0, 0, 0, h % per)
        )
    return pl.BlockSpec(
        (gw // width, far.shape[1], 2, BLK, width), lambda h, *f: (h, 0, 0, 0, 0)
    )


def attend(flags, queries, own, left, right, glob, rand, gw):
    rows, width = queries.shape
    steps = width // gw
    heads = width // HEAD_DIM
    per_step = gw // HEAD_DIM
    factor = 1.0 / math.sqrt(HEAD_DIM)
    q_spec = pl.BlockSpec((rows, gw), lambda h, *f: (0, h))
    p_spec = pl.BlockSpec((per_step, rows, HEAD_DIM), lambda h, *f: (h, 0, 0))
    s_spec = pl.BlockSpec((per_step, rows, 1), lambda h, *f: (h, 0, 0))
    part, m, d = pl.pallas_call(
        functools.partial(early_kernel, factor=factor),
        out_shape=(
            jax.ShapeDtypeStruct((heads, rows, HEAD_DIM), jnp.float32),
            jax.ShapeDtypeStruct((heads, rows, 1), jnp.float32),
            jax.ShapeDtypeStruct((heads, rows, 1), jnp.float32),
        ),
        grid_spec=pltpu.PrefetchScalarGridSpec(
            num_scalar_prefetch=1,
            grid=(steps,),
            in_specs=[
                q_spec,
                far_spec(own, gw),
                far_spec(left, gw),
                far_spec(right, gw),
                far_spec(glob, gw),
            ],
            out_specs=[p_spec, s_spec, s_spec],
        ),
    )(flags, queries, own, left, right, glob)
    return pl.pallas_call(
        functools.partial(late_kernel, factor=factor),
        out_shape=jax.ShapeDtypeStruct((rows, width), queries.dtype),
        grid=(steps,),
        in_specs=[q_spec, far_spec(rand, gw), p_spec, s_spec, s_spec],
        out_specs=q_spec,
    )(queries, rand, part, m, d)


def split_kernel(k_ref, v_ref, o_ref):
    piece = o_ref.shape[4]
    for j in range(o_ref.shape[0]):
        o_ref[j, 0, 0] = k_ref[:, pl.ds(j * piece, piece)]
        o_ref[j, 0, 1] = v_ref[:, pl.ds(j * piece, piece)]


def split_pieces(key_rows, values, peers):
    rows, width = key_rows.shape
    piece = width // peers
    if piece % HEAD_DIM:
        keyvals = jnp.stack((key_rows, values))
        return keyvals.reshape(2, rows, peers, piece).transpose(2, 0, 1, 3)[:, None]
    per = max(1, min(peers, SPLIT_WIDTH // piece))
    while peers % per:
        per -= 1
    return pl.pallas_call(
        split_kernel,
        out_shape=jax.ShapeDtypeStruct((peers, 1, 2, rows, piece), key_rows.dtype),
        grid=(peers // per,),
        in_specs=[
            pl.BlockSpec((rows, per * piece), lambda j: (0, j)),
            pl.BlockSpec((rows, per * piece), lambda j: (0, j)),
        ],
        out_specs=pl.BlockSpec((per, 1, 2, rows, piece), lambda j: (j, 0, 0, 0, 0)),
    )(key_rows, values)


def feature_major(far):
    peers, count, two, rows, piece = far.shape
    return far.transpose(1, 2, 3, 0, 4).reshape(1, count, two, rows, peers * piece)


def per_device(queries, key_rows, values, random_ids, global_ids):
    tok_rows, feat_width = queries.shape
    peers = lax.axis_size("seq")
    my_rank = lax.axis_index("seq")
    local_blocks = tok_rows // BLK
    assert local_blocks == 1
    all_blocks = local_blocks * peers
    piece = feat_width // peers
    pieces = split_pieces(key_rows, values, peers)
    spread = lax.all_to_all(pieces, "seq", split_axis=0, concat_axis=0, tiled=True)
    spread = spread.reshape(all_blocks, 2, BLK, piece)
    outgoing = jnp.take(spread, random_ids.reshape(-1), axis=0, mode="clip")
    outgoing = outgoing.reshape(all_blocks, RAND, 2, BLK, piece)
    left = shifted(pieces, "seq", 1)
    right = shifted(pieces, "seq", -1)
    outgoing, left, right = lax.optimization_barrier((outgoing, left, right))
    rand = lax.all_to_all(outgoing, "seq", split_axis=0, concat_axis=0, tiled=True)
    glob_piece = jnp.take(spread, global_ids, axis=0, mode="clip")
    glob = lax.all_gather(glob_piece[None], "seq", axis=0, tiled=True)
    flags = jnp.stack((my_rank > 0, my_rank < peers - 1)).astype(jnp.int32)
    if piece % HEAD_DIM == 0:
        gw = GROUP * HEAD_DIM if (GROUP * HEAD_DIM) % piece == 0 else piece
    else:
        glob = feature_major(glob)
        rand = feature_major(rand)
        gw = GROUP * HEAD_DIM
    own = pieces
    if piece % HEAD_DIM:
        own = feature_major(own)
        left = feature_major(left)
        right = feature_major(right)
    return attend(flags, queries, own, left, right, glob, rand, gw)


def solution(mesh):
    return jax.shard_map(
        per_device,
        mesh=mesh,
        in_specs=(
            P(("grp", "seq"), None),
            P(("grp", "seq"), None),
            P(("grp", "seq"), None),
            P("grp", None),
            P("grp"),
        ),
        out_specs=P(("grp", "seq"), None),
        check_vma=False,
    )
```

```python
import functools
import math

import jax
import jax.numpy as jnp
from jax import lax
from jax.experimental import pallas as pl
from jax.experimental.pallas import tpu as pltpu
from jax.sharding import PartitionSpec as P

HEADS = 32
HEAD_DIM = 128
BLK = 128
RAND = 3
GLOBAL = 2
GROUP = 8
SPLIT_WIDTH = 2048

neg_big = -1e30


def shifted(block, axis, step):
    count = lax.axis_size(axis)
    if step > 0:
        pairs = [(i, i + 1) for i in range(count - 1)]
    else:
        pairs = [(i + 1, i) for i in range(count - 1)]
    return lax.ppermute(block, axis, pairs)


def early_kernel(
    flags_ref, q_ref, own_ref, left_ref, right_ref, glob_ref, o_ref, m_ref, d_ref, *, factor
):
    left_ok = flags_ref[0] > 0
    right_ok = flags_ref[1] > 0
    keys = (3 + glob_ref.shape[1]) * BLK
    col = lax.broadcasted_iota(jnp.int32, (1, keys), 1)
    bad = ((col < BLK) & jnp.logical_not(left_ok)) | (
        (col >= 2 * BLK) & (col < 3 * BLK) & jnp.logical_not(right_ok)
    )
    bias = jnp.where(bad, neg_big, 0.0).astype(jnp.float32)
    piece_w = glob_ref.shape[4]
    for g in range(q_ref.shape[1] // HEAD_DIM):
        sl = pl.ds(g * HEAD_DIM, HEAD_DIM)
        src = (g * HEAD_DIM) // piece_w
        fsl = pl.ds((g * HEAD_DIM) % piece_w, HEAD_DIM)
        near = (left_ref, own_ref, right_ref)
        k_all = jnp.concatenate(
            (
                *[ref[src, 0, 0, :, fsl] for ref in near],
                *[glob_ref[src, j, 0, :, fsl] for j in range(glob_ref.shape[1])],
            ),
            axis=0,
        )
        scores = (
            lax.dot_general(
                q_ref[:, sl], k_all, (((1,), (1,)), ((), ())), preferred_element_type=jnp.float32
            )
            + bias
        )
        highest = jnp.max(scores, axis=-1, keepdims=True)
        weights = jnp.exp2((scores - highest) * factor)
        v_all = jnp.concatenate(
            (
                *[ref[src, 0, 1, :, fsl] for ref in near],
                *[glob_ref[src, j, 1, :, fsl] for j in range(glob_ref.shape[1])],
            ),
            axis=0,
        )
        o_ref[g] = jnp.dot(weights.astype(jnp.bfloat16), v_all, preferred_element_type=jnp.float32)
        m_ref[g] = highest
        d_ref[g] = jnp.sum(weights, axis=-1, keepdims=True)


def late_kernel(q_ref, rand_ref, part_ref, m_ref, d_ref, o_ref, *, factor):
    piece_w = rand_ref.shape[4]
    for g in range(q_ref.shape[1] // HEAD_DIM):
        sl = pl.ds(g * HEAD_DIM, HEAD_DIM)
        src = (g * HEAD_DIM) // piece_w
        fsl = pl.ds((g * HEAD_DIM) % piece_w, HEAD_DIM)
        count = rand_ref.shape[1]
        k_far = jnp.concatenate([rand_ref[src, j, 0, :, fsl] for j in range(count)], axis=0)
        v_far = jnp.concatenate([rand_ref[src, j, 1, :, fsl] for j in range(count)], axis=0)
        scores = lax.dot_general(
            q_ref[:, sl], k_far, (((1,), (1,)), ((), ())), preferred_element_type=jnp.float32
        )
        early_max = m_ref[g]
        highest = jnp.maximum(early_max, jnp.max(scores, axis=-1, keepdims=True))
        scale = jnp.exp2((early_max - highest) * factor)
        weights = jnp.exp2((scores - highest) * factor)
        denominator = d_ref[g] * scale + jnp.sum(weights, axis=-1, keepdims=True)
        mixed = part_ref[g] * scale + jnp.dot(
            weights.astype(jnp.bfloat16), v_far, preferred_element_type=jnp.float32
        )
        o_ref[:, sl] = (mixed / denominator).astype(o_ref.dtype)


def far_spec(far, gw):
    width = far.shape[4]
    if width >= gw:
        per = width // gw
        return pl.BlockSpec(
            (1, far.shape[1], 2, BLK, gw), lambda h, *f: (h // per, 0, 0, 0, h % per)
        )
    return pl.BlockSpec(
        (gw // width, far.shape[1], 2, BLK, width), lambda h, *f: (h, 0, 0, 0, 0)
    )


def attend(flags, queries, own, left, right, glob, rand, gw):
    rows, width = queries.shape
    steps = width // gw
    heads = width // HEAD_DIM
    per_step = gw // HEAD_DIM
    factor = math.log2(math.e) / math.sqrt(HEAD_DIM)
    q_spec = pl.BlockSpec((rows, gw), lambda h, *f: (0, h))
    p_spec = pl.BlockSpec((per_step, rows, HEAD_DIM), lambda h, *f: (h, 0, 0))
    s_spec = pl.BlockSpec((per_step, rows, 1), lambda h, *f: (h, 0, 0))
    part, m, d = pl.pallas_call(
        functools.partial(early_kernel, factor=factor),
        out_shape=(
            jax.ShapeDtypeStruct((heads, rows, HEAD_DIM), jnp.float32),
            jax.ShapeDtypeStruct((heads, rows, 1), jnp.float32),
            jax.ShapeDtypeStruct((heads, rows, 1), jnp.float32),
        ),
        grid_spec=pltpu.PrefetchScalarGridSpec(
            num_scalar_prefetch=1,
            grid=(steps,),
            in_specs=[
                q_spec,
                far_spec(own, gw),
                far_spec(left, gw),
                far_spec(right, gw),
                far_spec(glob, gw),
            ],
            out_specs=[p_spec, s_spec, s_spec],
        ),
    )(flags, queries, own, left, right, glob)
    return pl.pallas_call(
        functools.partial(late_kernel, factor=factor),
        out_shape=jax.ShapeDtypeStruct((rows, width), queries.dtype),
        grid=(steps,),
        in_specs=[q_spec, far_spec(rand, gw), p_spec, s_spec, s_spec],
        out_specs=q_spec,
    )(queries, rand, part, m, d)


def split_kernel(k_ref, v_ref, o_ref):
    piece = o_ref.shape[4]
    for j in range(o_ref.shape[0]):
        o_ref[j, 0, 0] = k_ref[:, pl.ds(j * piece, piece)]
        o_ref[j, 0, 1] = v_ref[:, pl.ds(j * piece, piece)]


def split_pieces(key_rows, values, peers):
    rows, width = key_rows.shape
    piece = width // peers
    if piece % HEAD_DIM:
        keyvals = jnp.stack((key_rows, values))
        return keyvals.reshape(2, rows, peers, piece).transpose(2, 0, 1, 3)[:, None]
    per = max(1, min(peers, SPLIT_WIDTH // piece))
    while peers % per:
        per -= 1
    return pl.pallas_call(
        split_kernel,
        out_shape=jax.ShapeDtypeStruct((peers, 1, 2, rows, piece), key_rows.dtype),
        grid=(peers // per,),
        in_specs=[
            pl.BlockSpec((rows, per * piece), lambda j: (0, j)),
            pl.BlockSpec((rows, per * piece), lambda j: (0, j)),
        ],
        out_specs=pl.BlockSpec((per, 1, 2, rows, piece), lambda j: (j, 0, 0, 0, 0)),
    )(key_rows, values)


def feature_major(far):
    peers, count, two, rows, piece = far.shape
    return far.transpose(1, 2, 3, 0, 4).reshape(1, count, two, rows, peers * piece)


def per_device(queries, key_rows, values, random_ids, global_ids):
    tok_rows, feat_width = queries.shape
    peers = lax.axis_size("seq")
    my_rank = lax.axis_index("seq")
    local_blocks = tok_rows // BLK
    assert local_blocks == 1
    all_blocks = local_blocks * peers
    piece = feat_width // peers
    pieces = split_pieces(key_rows, values, peers)
    spread = lax.all_to_all(pieces, "seq", split_axis=0, concat_axis=0, tiled=True)
    spread = spread.reshape(all_blocks, 2, BLK, piece)
    outgoing = jnp.take(spread, random_ids.reshape(-1), axis=0, mode="clip")
    outgoing = outgoing.reshape(all_blocks, RAND, 2, BLK, piece)
    left = shifted(pieces, "seq", 1)
    right = shifted(pieces, "seq", -1)
    outgoing, left, right = lax.optimization_barrier((outgoing, left, right))
    rand = lax.all_to_all(outgoing, "seq", split_axis=0, concat_axis=0, tiled=True)
    glob_piece = jnp.take(spread, global_ids, axis=0, mode="clip")
    glob = lax.all_gather(glob_piece[None], "seq", axis=0, tiled=True)
    flags = jnp.stack((my_rank > 0, my_rank < peers - 1)).astype(jnp.int32)
    if piece % HEAD_DIM == 0:
        gw = GROUP * HEAD_DIM if (GROUP * HEAD_DIM) % piece == 0 else piece
    else:
        glob = feature_major(glob)
        rand = feature_major(rand)
        gw = GROUP * HEAD_DIM
    own = pieces
    if piece % HEAD_DIM:
        own = feature_major(own)
        left = feature_major(left)
        right = feature_major(right)
    return attend(flags, queries, own, left, right, glob, rand, gw)


def solution(mesh):
    return jax.shard_map(
        per_device,
        mesh=mesh,
        in_specs=(
            P(("grp", "seq"), None),
            P(("grp", "seq"), None),
            P(("grp", "seq"), None),
            P("grp", None),
            P("grp"),
        ),
        out_specs=P(("grp", "seq"), None),
        check_vma=False,
    )
```

```python
import functools
import math

import jax
import jax.numpy as jnp
from jax import lax
from jax.experimental import pallas as pl
from jax.experimental.pallas import tpu as pltpu
from jax.sharding import PartitionSpec as P

HEADS = 32
HEAD_DIM = 128
BLK = 128
RAND = 3
GLOBAL = 2
GROUP = 4
SPLIT_WIDTH = 2048

neg_big = -1e30


def shifted(block, axis, step):
    count = lax.axis_size(axis)
    if step > 0:
        pairs = [(i, i + 1) for i in range(count - 1)]
    else:
        pairs = [(i + 1, i) for i in range(count - 1)]
    return lax.ppermute(block, axis, pairs)


def early_kernel(
    flags_ref, q_ref, own_ref, left_ref, right_ref, glob_ref, o_ref, m_ref, d_ref, *, factor
):
    left_ok = flags_ref[0] > 0
    right_ok = flags_ref[1] > 0
    keys = (3 + glob_ref.shape[1]) * BLK
    col = lax.broadcasted_iota(jnp.int32, (1, keys), 1)
    bad = ((col < BLK) & jnp.logical_not(left_ok)) | (
        (col >= 2 * BLK) & (col < 3 * BLK) & jnp.logical_not(right_ok)
    )
    bias = jnp.where(bad, neg_big, 0.0).astype(jnp.float32)
    piece_w = glob_ref.shape[4]
    for g in range(q_ref.shape[1] // HEAD_DIM):
        sl = pl.ds(g * HEAD_DIM, HEAD_DIM)
        src = (g * HEAD_DIM) // piece_w
        fsl = pl.ds((g * HEAD_DIM) % piece_w, HEAD_DIM)
        near = (left_ref, own_ref, right_ref)
        k_all = jnp.concatenate(
            (
                *[ref[src, 0, 0, :, fsl] for ref in near],
                *[glob_ref[src, j, 0, :, fsl] for j in range(glob_ref.shape[1])],
            ),
            axis=0,
        )
        scores = (
            lax.dot_general(
                q_ref[:, sl], k_all, (((1,), (1,)), ((), ())), preferred_element_type=jnp.float32
            )
            + bias
        )
        highest = jnp.max(scores, axis=-1, keepdims=True)
        weights = jnp.exp2((scores - highest) * factor)
        v_all = jnp.concatenate(
            (
                *[ref[src, 0, 1, :, fsl] for ref in near],
                *[glob_ref[src, j, 1, :, fsl] for j in range(glob_ref.shape[1])],
            ),
            axis=0,
        )
        o_ref[g] = jnp.dot(weights.astype(jnp.bfloat16), v_all, preferred_element_type=jnp.float32)
        m_ref[g] = highest
        d_ref[g] = jnp.sum(weights, axis=-1, keepdims=True)


def late_kernel(q_ref, rand_ref, part_ref, m_ref, d_ref, o_ref, *, factor):
    piece_w = rand_ref.shape[4]
    for g in range(q_ref.shape[1] // HEAD_DIM):
        sl = pl.ds(g * HEAD_DIM, HEAD_DIM)
        src = (g * HEAD_DIM) // piece_w
        fsl = pl.ds((g * HEAD_DIM) % piece_w, HEAD_DIM)
        count = rand_ref.shape[1]
        k_far = jnp.concatenate([rand_ref[src, j, 0, :, fsl] for j in range(count)], axis=0)
        v_far = jnp.concatenate([rand_ref[src, j, 1, :, fsl] for j in range(count)], axis=0)
        scores = lax.dot_general(
            q_ref[:, sl], k_far, (((1,), (1,)), ((), ())), preferred_element_type=jnp.float32
        )
        early_max = m_ref[g]
        highest = jnp.maximum(early_max, jnp.max(scores, axis=-1, keepdims=True))
        scale = jnp.exp2((early_max - highest) * factor)
        weights = jnp.exp2((scores - highest) * factor)
        denominator = d_ref[g] * scale + jnp.sum(weights, axis=-1, keepdims=True)
        mixed = part_ref[g] * scale + jnp.dot(
            weights.astype(jnp.bfloat16), v_far, preferred_element_type=jnp.float32
        )
        o_ref[:, sl] = (mixed / denominator).astype(o_ref.dtype)


def far_spec(far, gw):
    width = far.shape[4]
    if width >= gw:
        per = width // gw
        return pl.BlockSpec(
            (1, far.shape[1], 2, BLK, gw), lambda h, *f: (h // per, 0, 0, 0, h % per)
        )
    return pl.BlockSpec(
        (gw // width, far.shape[1], 2, BLK, width), lambda h, *f: (h, 0, 0, 0, 0)
    )


def attend(flags, queries, own, left, right, glob, rand, gw):
    rows, width = queries.shape
    steps = width // gw
    heads = width // HEAD_DIM
    per_step = gw // HEAD_DIM
    factor = math.log2(math.e) / math.sqrt(HEAD_DIM)
    q_spec = pl.BlockSpec((rows, gw), lambda h, *f: (0, h))
    p_spec = pl.BlockSpec((per_step, rows, HEAD_DIM), lambda h, *f: (h, 0, 0))
    s_spec = pl.BlockSpec((per_step, rows, 1), lambda h, *f: (h, 0, 0))
    part, m, d = pl.pallas_call(
        functools.partial(early_kernel, factor=factor),
        out_shape=(
            jax.ShapeDtypeStruct((heads, rows, HEAD_DIM), jnp.float32),
            jax.ShapeDtypeStruct((heads, rows, 1), jnp.float32),
            jax.ShapeDtypeStruct((heads, rows, 1), jnp.float32),
        ),
        grid_spec=pltpu.PrefetchScalarGridSpec(
            num_scalar_prefetch=1,
            grid=(steps,),
            in_specs=[
                q_spec,
                far_spec(own, gw),
                far_spec(left, gw),
                far_spec(right, gw),
                far_spec(glob, gw),
            ],
            out_specs=[p_spec, s_spec, s_spec],
        ),
    )(flags, queries, own, left, right, glob)
    return pl.pallas_call(
        functools.partial(late_kernel, factor=factor),
        out_shape=jax.ShapeDtypeStruct((rows, width), queries.dtype),
        grid=(steps,),
        in_specs=[q_spec, far_spec(rand, gw), p_spec, s_spec, s_spec],
        out_specs=q_spec,
    )(queries, rand, part, m, d)


def split_kernel(k_ref, v_ref, o_ref):
    piece = o_ref.shape[4]
    for j in range(o_ref.shape[0]):
        o_ref[j, 0, 0] = k_ref[:, pl.ds(j * piece, piece)]
        o_ref[j, 0, 1] = v_ref[:, pl.ds(j * piece, piece)]


def split_pieces(key_rows, values, peers):
    rows, width = key_rows.shape
    piece = width // peers
    if piece % HEAD_DIM:
        keyvals = jnp.stack((key_rows, values))
        return keyvals.reshape(2, rows, peers, piece).transpose(2, 0, 1, 3)[:, None]
    per = max(1, min(peers, SPLIT_WIDTH // piece))
    while peers % per:
        per -= 1
    return pl.pallas_call(
        split_kernel,
        out_shape=jax.ShapeDtypeStruct((peers, 1, 2, rows, piece), key_rows.dtype),
        grid=(peers // per,),
        in_specs=[
            pl.BlockSpec((rows, per * piece), lambda j: (0, j)),
            pl.BlockSpec((rows, per * piece), lambda j: (0, j)),
        ],
        out_specs=pl.BlockSpec((per, 1, 2, rows, piece), lambda j: (j, 0, 0, 0, 0)),
    )(key_rows, values)


def feature_major(far):
    peers, count, two, rows, piece = far.shape
    return far.transpose(1, 2, 3, 0, 4).reshape(1, count, two, rows, peers * piece)


def per_device(queries, key_rows, values, random_ids, global_ids):
    tok_rows, feat_width = queries.shape
    peers = lax.axis_size("seq")
    my_rank = lax.axis_index("seq")
    local_blocks = tok_rows // BLK
    assert local_blocks == 1
    all_blocks = local_blocks * peers
    piece = feat_width // peers
    pieces = split_pieces(key_rows, values, peers)
    spread = lax.all_to_all(pieces, "seq", split_axis=0, concat_axis=0, tiled=True)
    spread = spread.reshape(all_blocks, 2, BLK, piece)
    outgoing = jnp.take(spread, random_ids.reshape(-1), axis=0, mode="clip")
    outgoing = outgoing.reshape(all_blocks, RAND, 2, BLK, piece)
    left = shifted(pieces, "seq", 1)
    right = shifted(pieces, "seq", -1)
    outgoing, left, right = lax.optimization_barrier((outgoing, left, right))
    rand = lax.all_to_all(outgoing, "seq", split_axis=0, concat_axis=0, tiled=True)
    glob_piece = jnp.take(spread, global_ids, axis=0, mode="clip")
    glob = lax.all_gather(glob_piece[None], "seq", axis=0, tiled=True)
    flags = jnp.stack((my_rank > 0, my_rank < peers - 1)).astype(jnp.int32)
    if piece % HEAD_DIM == 0:
        gw = GROUP * HEAD_DIM if (GROUP * HEAD_DIM) % piece == 0 else piece
    else:
        glob = feature_major(glob)
        rand = feature_major(rand)
        gw = GROUP * HEAD_DIM
    own = pieces
    if piece % HEAD_DIM:
        own = feature_major(own)
        left = feature_major(left)
        right = feature_major(right)
    return attend(flags, queries, own, left, right, glob, rand, gw)


def solution(mesh):
    return jax.shard_map(
        per_device,
        mesh=mesh,
        in_specs=(
            P(("grp", "seq"), None),
            P(("grp", "seq"), None),
            P(("grp", "seq"), None),
            P("grp", None),
            P("grp"),
        ),
        out_specs=P(("grp", "seq"), None),
        check_vma=False,
    )
```

```python
import functools
import math

import jax
import jax.numpy as jnp
from jax import lax
from jax.experimental import pallas as pl
from jax.experimental.pallas import tpu as pltpu
from jax.sharding import PartitionSpec as P

HEADS = 32
HEAD_DIM = 128
BLK = 128
RAND = 3
GLOBAL = 2
GROUP = 8
SPLIT_WIDTH = 2048

neg_big = -1e30


def shifted(block, axis, step):
    count = lax.axis_size(axis)
    if step > 0:
        pairs = [(i, i + 1) for i in range(count - 1)]
    else:
        pairs = [(i + 1, i) for i in range(count - 1)]
    return lax.ppermute(block, axis, pairs)


def early_kernel(
    flags_ref, q_ref, own_ref, left_ref, right_ref, glob_ref, o_ref, m_ref, d_ref, *, factor
):
    left_ok = flags_ref[0] > 0
    right_ok = flags_ref[1] > 0
    keys = (3 + glob_ref.shape[1]) * BLK
    col = lax.broadcasted_iota(jnp.int32, (1, keys), 1)
    bad = ((col < BLK) & jnp.logical_not(left_ok)) | (
        (col >= 2 * BLK) & (col < 3 * BLK) & jnp.logical_not(right_ok)
    )
    bias = jnp.where(bad, neg_big, 0.0).astype(jnp.float32)
    piece_w = glob_ref.shape[4]
    for g in range(q_ref.shape[1] // HEAD_DIM):
        sl = pl.ds(g * HEAD_DIM, HEAD_DIM)
        src = (g * HEAD_DIM) // piece_w
        fsl = pl.ds((g * HEAD_DIM) % piece_w, HEAD_DIM)
        near = (left_ref, own_ref, right_ref)
        k_all = jnp.concatenate(
            (
                *[ref[src, 0, 0, :, fsl] for ref in near],
                *[glob_ref[src, j, 0, :, fsl] for j in range(glob_ref.shape[1])],
            ),
            axis=0,
        )
        scores = (
            lax.dot_general(
                q_ref[:, sl], k_all, (((1,), (1,)), ((), ())), preferred_element_type=jnp.float32
            )
            + bias
        )
        highest = jnp.max(scores, axis=-1, keepdims=True)
        weights = jnp.exp2((scores - highest) * factor)
        v_all = jnp.concatenate(
            (
                *[ref[src, 0, 1, :, fsl] for ref in near],
                *[glob_ref[src, j, 1, :, fsl] for j in range(glob_ref.shape[1])],
            ),
            axis=0,
        )
        o_ref[g] = jnp.dot(weights.astype(jnp.bfloat16), v_all, preferred_element_type=jnp.float32)
        m_ref[g] = highest
        d_ref[g] = jnp.sum(weights, axis=-1, keepdims=True)


def late_kernel(q_ref, rand_ref, part_ref, m_ref, d_ref, o_ref, *, factor):
    piece_w = rand_ref.shape[4]
    for g in range(q_ref.shape[1] // HEAD_DIM):
        sl = pl.ds(g * HEAD_DIM, HEAD_DIM)
        src = (g * HEAD_DIM) // piece_w
        fsl = pl.ds((g * HEAD_DIM) % piece_w, HEAD_DIM)
        count = rand_ref.shape[1]
        k_far = jnp.concatenate([rand_ref[src, j, 0, :, fsl] for j in range(count)], axis=0)
        v_far = jnp.concatenate([rand_ref[src, j, 1, :, fsl] for j in range(count)], axis=0)
        scores = lax.dot_general(
            q_ref[:, sl], k_far, (((1,), (1,)), ((), ())), preferred_element_type=jnp.float32
        )
        early_max = m_ref[g]
        highest = jnp.maximum(early_max, jnp.max(scores, axis=-1, keepdims=True))
        scale = jnp.exp2((early_max - highest) * factor)
        weights = jnp.exp2((scores - highest) * factor)
        denominator = d_ref[g] * scale + jnp.sum(weights, axis=-1, keepdims=True)
        mixed = part_ref[g] * scale + jnp.dot(
            weights.astype(jnp.bfloat16), v_far, preferred_element_type=jnp.float32
        )
        o_ref[:, sl] = (mixed / denominator).astype(o_ref.dtype)


def far_spec(far, gw):
    width = far.shape[4]
    if width >= gw:
        per = width // gw
        return pl.BlockSpec(
            (1, far.shape[1], 2, BLK, gw), lambda h, *f: (h // per, 0, 0, 0, h % per)
        )
    return pl.BlockSpec(
        (gw // width, far.shape[1], 2, BLK, width), lambda h, *f: (h, 0, 0, 0, 0)
    )


def attend(flags, queries, own, left, right, glob, rand, gw):
    rows, width = queries.shape
    steps = width // gw
    heads = width // HEAD_DIM
    per_step = gw // HEAD_DIM
    factor = math.log2(math.e) / math.sqrt(HEAD_DIM)
    q_spec = pl.BlockSpec((rows, gw), lambda h, *f: (0, h))
    p_spec = pl.BlockSpec((per_step, rows, HEAD_DIM), lambda h, *f: (h, 0, 0))
    s_spec = pl.BlockSpec((per_step, rows, 1), lambda h, *f: (h, 0, 0))
    part, m, d = pl.pallas_call(
        functools.partial(early_kernel, factor=factor),
        out_shape=(
            jax.ShapeDtypeStruct((heads, rows, HEAD_DIM), jnp.float32),
            jax.ShapeDtypeStruct((heads, rows, 1), jnp.float32),
            jax.ShapeDtypeStruct((heads, rows, 1), jnp.float32),
        ),
        grid_spec=pltpu.PrefetchScalarGridSpec(
            num_scalar_prefetch=1,
            grid=(steps,),
            in_specs=[
                q_spec,
                far_spec(own, gw),
                far_spec(left, gw),
                far_spec(right, gw),
                far_spec(glob, gw),
            ],
            out_specs=[p_spec, s_spec, s_spec],
        ),
    )(flags, queries, own, left, right, glob)
    return pl.pallas_call(
        functools.partial(late_kernel, factor=factor),
        out_shape=jax.ShapeDtypeStruct((rows, width), queries.dtype),
        grid=(steps,),
        in_specs=[q_spec, far_spec(rand, gw), p_spec, s_spec, s_spec],
        out_specs=q_spec,
    )(queries, rand, part, m, d)


def split_kernel(k_ref, v_ref, o_ref):
    piece = o_ref.shape[4]
    for j in range(o_ref.shape[0]):
        o_ref[j, 0, 0] = k_ref[:, pl.ds(j * piece, piece)]
        o_ref[j, 0, 1] = v_ref[:, pl.ds(j * piece, piece)]


def split_pieces(key_rows, values, peers):
    rows, width = key_rows.shape
    piece = width // peers
    if piece % HEAD_DIM:
        keyvals = jnp.stack((key_rows, values))
        return keyvals.reshape(2, rows, peers, piece).transpose(2, 0, 1, 3)[:, None]
    per = max(1, min(peers, SPLIT_WIDTH // piece))
    while peers % per:
        per -= 1
    return pl.pallas_call(
        split_kernel,
        out_shape=jax.ShapeDtypeStruct((peers, 1, 2, rows, piece), key_rows.dtype),
        grid=(peers // per,),
        in_specs=[
            pl.BlockSpec((rows, per * piece), lambda j: (0, j)),
            pl.BlockSpec((rows, per * piece), lambda j: (0, j)),
        ],
        out_specs=pl.BlockSpec((per, 1, 2, rows, piece), lambda j: (j, 0, 0, 0, 0)),
    )(key_rows, values)


def feature_major(far):
    peers, count, two, rows, piece = far.shape
    return far.transpose(1, 2, 3, 0, 4).reshape(1, count, two, rows, peers * piece)


def per_device(queries, key_rows, values, random_ids, global_ids):
    tok_rows, feat_width = queries.shape
    peers = lax.axis_size("seq")
    my_rank = lax.axis_index("seq")
    local_blocks = tok_rows // BLK
    assert local_blocks == 1
    all_blocks = local_blocks * peers
    piece = feat_width // peers
    pieces = split_pieces(key_rows, values, peers)
    spread = lax.all_to_all(pieces, "seq", split_axis=0, concat_axis=0, tiled=True)
    spread = spread.reshape(all_blocks, 2, BLK, piece)
    outgoing = jnp.take(spread, random_ids.reshape(-1), axis=0, mode="clip")
    outgoing = outgoing.reshape(all_blocks, RAND, 2, BLK, piece)
    left = shifted(pieces, "seq", 1)
    right = shifted(pieces, "seq", -1)
    rand = lax.all_to_all(outgoing, "seq", split_axis=0, concat_axis=0, tiled=True)
    glob_piece = jnp.take(spread, global_ids, axis=0, mode="clip")
    glob = lax.all_gather(glob_piece[None], "seq", axis=0, tiled=True)
    flags = jnp.stack((my_rank > 0, my_rank < peers - 1)).astype(jnp.int32)
    if piece % HEAD_DIM == 0:
        gw = GROUP * HEAD_DIM if (GROUP * HEAD_DIM) % piece == 0 else piece
    else:
        glob = feature_major(glob)
        rand = feature_major(rand)
        gw = GROUP * HEAD_DIM
    own = pieces
    if piece % HEAD_DIM:
        own = feature_major(own)
        left = feature_major(left)
        right = feature_major(right)
    return attend(flags, queries, own, left, right, glob, rand, gw)


def solution(mesh):
    return jax.shard_map(
        per_device,
        mesh=mesh,
        in_specs=(
            P(("grp", "seq"), None),
            P(("grp", "seq"), None),
            P(("grp", "seq"), None),
            P("grp", None),
            P("grp"),
        ),
        out_specs=P(("grp", "seq"), None),
        check_vma=False,
    )
```

```python
import functools
import math

import jax
import jax.numpy as jnp
from jax import lax
from jax.experimental import pallas as pl
from jax.experimental.pallas import tpu as pltpu
from jax.sharding import PartitionSpec as P

HEADS = 32
HEAD_DIM = 128
BLK = 128
RAND = 3
GLOBAL = 2
GROUP = 8
SPLIT_WIDTH = 4096

neg_big = -1e30


def shifted(block, axis, step):
    count = lax.axis_size(axis)
    if step > 0:
        pairs = [(i, i + 1) for i in range(count - 1)]
    else:
        pairs = [(i + 1, i) for i in range(count - 1)]
    return lax.ppermute(block, axis, pairs)


def early_kernel(
    flags_ref, q_ref, own_ref, left_ref, right_ref, glob_ref, o_ref, m_ref, d_ref, *, factor
):
    left_ok = flags_ref[0] > 0
    right_ok = flags_ref[1] > 0
    keys = (3 + glob_ref.shape[1]) * BLK
    col = lax.broadcasted_iota(jnp.int32, (1, keys), 1)
    bad = ((col < BLK) & jnp.logical_not(left_ok)) | (
        (col >= 2 * BLK) & (col < 3 * BLK) & jnp.logical_not(right_ok)
    )
    bias = jnp.where(bad, neg_big, 0.0).astype(jnp.float32)
    piece_w = glob_ref.shape[4]
    for g in range(q_ref.shape[1] // HEAD_DIM):
        sl = pl.ds(g * HEAD_DIM, HEAD_DIM)
        src = (g * HEAD_DIM) // piece_w
        fsl = pl.ds((g * HEAD_DIM) % piece_w, HEAD_DIM)
        near = (left_ref, own_ref, right_ref)
        k_all = jnp.concatenate(
            (
                *[ref[src, 0, 0, :, fsl] for ref in near],
                *[glob_ref[src, j, 0, :, fsl] for j in range(glob_ref.shape[1])],
            ),
            axis=0,
        )
        scores = (
            lax.dot_general(
                q_ref[:, sl], k_all, (((1,), (1,)), ((), ())), preferred_element_type=jnp.float32
            )
            + bias
        )
        highest = jnp.max(scores, axis=-1, keepdims=True)
        weights = jnp.exp2((scores - highest) * factor)
        v_all = jnp.concatenate(
            (
                *[ref[src, 0, 1, :, fsl] for ref in near],
                *[glob_ref[src, j, 1, :, fsl] for j in range(glob_ref.shape[1])],
            ),
            axis=0,
        )
        o_ref[g] = jnp.dot(weights.astype(jnp.bfloat16), v_all, preferred_element_type=jnp.float32)
        m_ref[g] = highest
        d_ref[g] = jnp.sum(weights, axis=-1, keepdims=True)


def late_kernel(q_ref, rand_ref, part_ref, m_ref, d_ref, o_ref, *, factor):
    piece_w = rand_ref.shape[4]
    for g in range(q_ref.shape[1] // HEAD_DIM):
        sl = pl.ds(g * HEAD_DIM, HEAD_DIM)
        src = (g * HEAD_DIM) // piece_w
        fsl = pl.ds((g * HEAD_DIM) % piece_w, HEAD_DIM)
        count = rand_ref.shape[1]
        k_far = jnp.concatenate([rand_ref[src, j, 0, :, fsl] for j in range(count)], axis=0)
        v_far = jnp.concatenate([rand_ref[src, j, 1, :, fsl] for j in range(count)], axis=0)
        scores = lax.dot_general(
            q_ref[:, sl], k_far, (((1,), (1,)), ((), ())), preferred_element_type=jnp.float32
        )
        early_max = m_ref[g]
        highest = jnp.maximum(early_max, jnp.max(scores, axis=-1, keepdims=True))
        scale = jnp.exp2((early_max - highest) * factor)
        weights = jnp.exp2((scores - highest) * factor)
        denominator = d_ref[g] * scale + jnp.sum(weights, axis=-1, keepdims=True)
        mixed = part_ref[g] * scale + jnp.dot(
            weights.astype(jnp.bfloat16), v_far, preferred_element_type=jnp.float32
        )
        o_ref[:, sl] = (mixed / denominator).astype(o_ref.dtype)


def far_spec(far, gw):
    width = far.shape[4]
    if width >= gw:
        per = width // gw
        return pl.BlockSpec(
            (1, far.shape[1], 2, BLK, gw), lambda h, *f: (h // per, 0, 0, 0, h % per)
        )
    return pl.BlockSpec(
        (gw // width, far.shape[1], 2, BLK, width), lambda h, *f: (h, 0, 0, 0, 0)
    )


def attend(flags, queries, own, left, right, glob, rand, gw):
    rows, width = queries.shape
    steps = width // gw
    heads = width // HEAD_DIM
    per_step = gw // HEAD_DIM
    factor = math.log2(math.e) / math.sqrt(HEAD_DIM)
    q_spec = pl.BlockSpec((rows, gw), lambda h, *f: (0, h))
    p_spec = pl.BlockSpec((per_step, rows, HEAD_DIM), lambda h, *f: (h, 0, 0))
    s_spec = pl.BlockSpec((per_step, rows, 1), lambda h, *f: (h, 0, 0))
    part, m, d = pl.pallas_call(
        functools.partial(early_kernel, factor=factor),
        out_shape=(
            jax.ShapeDtypeStruct((heads, rows, HEAD_DIM), jnp.float32),
            jax.ShapeDtypeStruct((heads, rows, 1), jnp.float32),
            jax.ShapeDtypeStruct((heads, rows, 1), jnp.float32),
        ),
        grid_spec=pltpu.PrefetchScalarGridSpec(
            num_scalar_prefetch=1,
            grid=(steps,),
            in_specs=[
                q_spec,
                far_spec(own, gw),
                far_spec(left, gw),
                far_spec(right, gw),
                far_spec(glob, gw),
            ],
            out_specs=[p_spec, s_spec, s_spec],
        ),
    )(flags, queries, own, left, right, glob)
    return pl.pallas_call(
        functools.partial(late_kernel, factor=factor),
        out_shape=jax.ShapeDtypeStruct((rows, width), queries.dtype),
        grid=(steps,),
        in_specs=[q_spec, far_spec(rand, gw), p_spec, s_spec, s_spec],
        out_specs=q_spec,
    )(queries, rand, part, m, d)


def split_kernel(k_ref, v_ref, o_ref):
    piece = o_ref.shape[4]
    for j in range(o_ref.shape[0]):
        o_ref[j, 0, 0] = k_ref[:, pl.ds(j * piece, piece)]
        o_ref[j, 0, 1] = v_ref[:, pl.ds(j * piece, piece)]


def split_pieces(key_rows, values, peers):
    rows, width = key_rows.shape
    piece = width // peers
    if piece % HEAD_DIM:
        keyvals = jnp.stack((key_rows, values))
        return keyvals.reshape(2, rows, peers, piece).transpose(2, 0, 1, 3)[:, None]
    per = max(1, min(peers, SPLIT_WIDTH // piece))
    while peers % per:
        per -= 1
    return pl.pallas_call(
        split_kernel,
        out_shape=jax.ShapeDtypeStruct((peers, 1, 2, rows, piece), key_rows.dtype),
        grid=(peers // per,),
        in_specs=[
            pl.BlockSpec((rows, per * piece), lambda j: (0, j)),
            pl.BlockSpec((rows, per * piece), lambda j: (0, j)),
        ],
        out_specs=pl.BlockSpec((per, 1, 2, rows, piece), lambda j: (j, 0, 0, 0, 0)),
    )(key_rows, values)


def feature_major(far):
    peers, count, two, rows, piece = far.shape
    return far.transpose(1, 2, 3, 0, 4).reshape(1, count, two, rows, peers * piece)


def per_device(queries, key_rows, values, random_ids, global_ids):
    tok_rows, feat_width = queries.shape
    peers = lax.axis_size("seq")
    my_rank = lax.axis_index("seq")
    local_blocks = tok_rows // BLK
    assert local_blocks == 1
    all_blocks = local_blocks * peers
    piece = feat_width // peers
    pieces = split_pieces(key_rows, values, peers)
    spread = lax.all_to_all(pieces, "seq", split_axis=0, concat_axis=0, tiled=True)
    spread = spread.reshape(all_blocks, 2, BLK, piece)
    outgoing = jnp.take(spread, random_ids.reshape(-1), axis=0, mode="clip")
    outgoing = outgoing.reshape(all_blocks, RAND, 2, BLK, piece)
    left = shifted(pieces, "seq", 1)
    right = shifted(pieces, "seq", -1)
    outgoing, left, right = lax.optimization_barrier((outgoing, left, right))
    rand = lax.all_to_all(outgoing, "seq", split_axis=0, concat_axis=0, tiled=True)
    glob_piece = jnp.take(spread, global_ids, axis=0, mode="clip")
    glob = lax.all_gather(glob_piece[None], "seq", axis=0, tiled=True)
    flags = jnp.stack((my_rank > 0, my_rank < peers - 1)).astype(jnp.int32)
    if piece % HEAD_DIM == 0:
        gw = GROUP * HEAD_DIM if (GROUP * HEAD_DIM) % piece == 0 else piece
    else:
        glob = feature_major(glob)
        rand = feature_major(rand)
        gw = GROUP * HEAD_DIM
    own = pieces
    if piece % HEAD_DIM:
        own = feature_major(own)
        left = feature_major(left)
        right = feature_major(right)
    return attend(flags, queries, own, left, right, glob, rand, gw)


def solution(mesh):
    return jax.shard_map(
        per_device,
        mesh=mesh,
        in_specs=(
            P(("grp", "seq"), None),
            P(("grp", "seq"), None),
            P(("grp", "seq"), None),
            P("grp", None),
            P("grp"),
        ),
        out_specs=P(("grp", "seq"), None),
        check_vma=False,
    )
```

```python
import functools
import math

import jax
import jax.numpy as jnp
from jax import lax
from jax.experimental import pallas as pl
from jax.experimental.pallas import tpu as pltpu
from jax.sharding import PartitionSpec as P

HEADS = 32
HEAD_DIM = 128
BLK = 128
RAND = 3
GLOBAL = 2
GROUP = 8
SPLIT_WIDTH = 2048

neg_big = -1e30


def shifted(block, axis, step):
    count = lax.axis_size(axis)
    if step > 0:
        pairs = [(i, i + 1) for i in range(count - 1)]
    else:
        pairs = [(i + 1, i) for i in range(count - 1)]
    return lax.ppermute(block, axis, pairs)


def early_kernel(
    flags_ref, q_ref, own_ref, left_ref, right_ref, glob_ref, o_ref, m_ref, d_ref, *, factor
):
    left_ok = flags_ref[0] > 0
    right_ok = flags_ref[1] > 0
    keys = (3 + glob_ref.shape[1]) * BLK
    col = lax.broadcasted_iota(jnp.int32, (1, keys), 1)
    bad = ((col < BLK) & jnp.logical_not(left_ok)) | (
        (col >= 2 * BLK) & (col < 3 * BLK) & jnp.logical_not(right_ok)
    )
    bias = jnp.where(bad, neg_big, 0.0).astype(jnp.float32)
    piece_w = glob_ref.shape[4]
    for g in range(q_ref.shape[1] // HEAD_DIM):
        sl = pl.ds(g * HEAD_DIM, HEAD_DIM)
        src = (g * HEAD_DIM) // piece_w
        fsl = pl.ds((g * HEAD_DIM) % piece_w, HEAD_DIM)
        near = (left_ref, own_ref, right_ref)
        k_all = jnp.concatenate(
            (
                *[ref[src, 0, 0, :, fsl] for ref in near],
                *[glob_ref[src, j, 0, :, fsl] for j in range(glob_ref.shape[1])],
            ),
            axis=0,
        )
        scores = (
            lax.dot_general(
                q_ref[:, sl], k_all, (((1,), (1,)), ((), ())), preferred_element_type=jnp.float32
            )
            + bias
        )
        highest = jnp.max(scores, axis=-1, keepdims=True)
        weights = jnp.exp2((scores - highest) * factor)
        v_all = jnp.concatenate(
            (
                *[ref[src, 0, 1, :, fsl] for ref in near],
                *[glob_ref[src, j, 1, :, fsl] for j in range(glob_ref.shape[1])],
            ),
            axis=0,
        )
        o_ref[g] = jnp.dot(weights.astype(jnp.bfloat16), v_all, preferred_element_type=jnp.float32)
        m_ref[g] = highest
        d_ref[g] = jnp.sum(weights, axis=-1, keepdims=True)


def late_kernel(q_ref, rand_ref, part_ref, m_ref, d_ref, o_ref, *, factor):
    piece_w = rand_ref.shape[4]
    for g in range(q_ref.shape[1] // HEAD_DIM):
        sl = pl.ds(g * HEAD_DIM, HEAD_DIM)
        src = (g * HEAD_DIM) // piece_w
        fsl = pl.ds((g * HEAD_DIM) % piece_w, HEAD_DIM)
        count = rand_ref.shape[1]
        k_far = jnp.concatenate([rand_ref[src, j, 0, :, fsl] for j in range(count)], axis=0)
        v_far = jnp.concatenate([rand_ref[src, j, 1, :, fsl] for j in range(count)], axis=0)
        scores = lax.dot_general(
            q_ref[:, sl], k_far, (((1,), (1,)), ((), ())), preferred_element_type=jnp.float32
        )
        early_max = m_ref[g]
        highest = jnp.maximum(early_max, jnp.max(scores, axis=-1, keepdims=True))
        scale = jnp.exp2((early_max - highest) * factor)
        weights = jnp.exp2((scores - highest) * factor)
        denominator = d_ref[g] * scale + jnp.sum(weights, axis=-1, keepdims=True)
        mixed = part_ref[g] * scale + jnp.dot(
            weights.astype(jnp.bfloat16), v_far, preferred_element_type=jnp.float32
        )
        o_ref[:, sl] = (mixed * (1.0 / denominator)).astype(o_ref.dtype)


def far_spec(far, gw):
    width = far.shape[4]
    if width >= gw:
        per = width // gw
        return pl.BlockSpec(
            (1, far.shape[1], 2, BLK, gw), lambda h, *f: (h // per, 0, 0, 0, h % per)
        )
    return pl.BlockSpec(
        (gw // width, far.shape[1], 2, BLK, width), lambda h, *f: (h, 0, 0, 0, 0)
    )


def attend(flags, queries, own, left, right, glob, rand, gw):
    rows, width = queries.shape
    steps = width // gw
    heads = width // HEAD_DIM
    per_step = gw // HEAD_DIM
    factor = math.log2(math.e) / math.sqrt(HEAD_DIM)
    q_spec = pl.BlockSpec((rows, gw), lambda h, *f: (0, h))
    p_spec = pl.BlockSpec((per_step, rows, HEAD_DIM), lambda h, *f: (h, 0, 0))
    s_spec = pl.BlockSpec((per_step, rows, 1), lambda h, *f: (h, 0, 0))
    part, m, d = pl.pallas_call(
        functools.partial(early_kernel, factor=factor),
        out_shape=(
            jax.ShapeDtypeStruct((heads, rows, HEAD_DIM), jnp.float32),
            jax.ShapeDtypeStruct((heads, rows, 1), jnp.float32),
            jax.ShapeDtypeStruct((heads, rows, 1), jnp.float32),
        ),
        grid_spec=pltpu.PrefetchScalarGridSpec(
            num_scalar_prefetch=1,
            grid=(steps,),
            in_specs=[
                q_spec,
                far_spec(own, gw),
                far_spec(left, gw),
                far_spec(right, gw),
                far_spec(glob, gw),
            ],
            out_specs=[p_spec, s_spec, s_spec],
        ),
    )(flags, queries, own, left, right, glob)
    return pl.pallas_call(
        functools.partial(late_kernel, factor=factor),
        out_shape=jax.ShapeDtypeStruct((rows, width), queries.dtype),
        grid=(steps,),
        in_specs=[q_spec, far_spec(rand, gw), p_spec, s_spec, s_spec],
        out_specs=q_spec,
    )(queries, rand, part, m, d)


def split_kernel(k_ref, v_ref, o_ref):
    piece = o_ref.shape[4]
    for j in range(o_ref.shape[0]):
        o_ref[j, 0, 0] = k_ref[:, pl.ds(j * piece, piece)]
        o_ref[j, 0, 1] = v_ref[:, pl.ds(j * piece, piece)]


def split_pieces(key_rows, values, peers):
    rows, width = key_rows.shape
    piece = width // peers
    if piece % HEAD_DIM:
        keyvals = jnp.stack((key_rows, values))
        return keyvals.reshape(2, rows, peers, piece).transpose(2, 0, 1, 3)[:, None]
    per = max(1, min(peers, SPLIT_WIDTH // piece))
    while peers % per:
        per -= 1
    return pl.pallas_call(
        split_kernel,
        out_shape=jax.ShapeDtypeStruct((peers, 1, 2, rows, piece), key_rows.dtype),
        grid=(peers // per,),
        in_specs=[
            pl.BlockSpec((rows, per * piece), lambda j: (0, j)),
            pl.BlockSpec((rows, per * piece), lambda j: (0, j)),
        ],
        out_specs=pl.BlockSpec((per, 1, 2, rows, piece), lambda j: (j, 0, 0, 0, 0)),
    )(key_rows, values)


def feature_major(far):
    peers, count, two, rows, piece = far.shape
    return far.transpose(1, 2, 3, 0, 4).reshape(1, count, two, rows, peers * piece)


def per_device(queries, key_rows, values, random_ids, global_ids):
    tok_rows, feat_width = queries.shape
    peers = lax.axis_size("seq")
    my_rank = lax.axis_index("seq")
    local_blocks = tok_rows // BLK
    assert local_blocks == 1
    all_blocks = local_blocks * peers
    piece = feat_width // peers
    pieces = split_pieces(key_rows, values, peers)
    spread = lax.all_to_all(pieces, "seq", split_axis=0, concat_axis=0, tiled=True)
    spread = spread.reshape(all_blocks, 2, BLK, piece)
    outgoing = jnp.take(spread, random_ids.reshape(-1), axis=0, mode="clip")
    outgoing = outgoing.reshape(all_blocks, RAND, 2, BLK, piece)
    left = shifted(pieces, "seq", 1)
    right = shifted(pieces, "seq", -1)
    outgoing, left, right = lax.optimization_barrier((outgoing, left, right))
    rand = lax.all_to_all(outgoing, "seq", split_axis=0, concat_axis=0, tiled=True)
    glob_piece = jnp.take(spread, global_ids, axis=0, mode="clip")
    glob = lax.all_gather(glob_piece[None], "seq", axis=0, tiled=True)
    flags = jnp.stack((my_rank > 0, my_rank < peers - 1)).astype(jnp.int32)
    if piece % HEAD_DIM == 0:
        gw = GROUP * HEAD_DIM if (GROUP * HEAD_DIM) % piece == 0 else piece
    else:
        glob = feature_major(glob)
        rand = feature_major(rand)
        gw = GROUP * HEAD_DIM
    own = pieces
    if piece % HEAD_DIM:
        own = feature_major(own)
        left = feature_major(left)
        right = feature_major(right)
    return attend(flags, queries, own, left, right, glob, rand, gw)


def solution(mesh):
    return jax.shard_map(
        per_device,
        mesh=mesh,
        in_specs=(
            P(("grp", "seq"), None),
            P(("grp", "seq"), None),
            P(("grp", "seq"), None),
            P("grp", None),
            P("grp"),
        ),
        out_specs=P(("grp", "seq"), None),
        check_vma=False,
    )
```
